128 devices in a mesh: srow: 8 (over y_lo, z), scol: 16 (over y_hi, x, core).
Axes of the slice: x: 4, y: 4 (y_hi: 2, y_lo: 2; y = y_hi * 2 + y_lo), z: 4, core: 2. Of those that a mesh axis runs over, the one named last changes fastest.
Arguments:
- frames: bfloat16 [512, 1024, 256], P('srow', 'scol'), may hold values from 0.19921875 to 1.796875
- pixel_gain: float32 [256], replicated, may hold values from 0.5 to 1.5
- eigen_flats: float32 [16, 256], replicated, may hold values from -0.375 to 0.375
- pixels: int32 [256], replicated, may hold values from 0 to 1023, as said below
Outputs:
- object_wave: float32 [512, 2, 1024], P('scol', None, 'srow')
The draws below stay inside these ranges and needn't reach their ends.
Inputs may be any that keep to these rules, and one draw needn't show every extreme that they name: Distinct indices y * 32 + x of detector pixels whose centre offset (x - 16, y - 16) lies within 13 pixels.
All inputs are finite; a program needn't handle non-finite values.
Results may differ from the reference program's by a relative error of at most 0.011.
Values may be sent and summed in bfloat16 or wider, within the bound.
No kernel may reach another device: no remote copies, remote signals or barrier semaphores. Data moves between devices by JAX's collectives and lax.ppermute only.
A program may use at most 128 MiB of HBM per device.

```python
import math
import jax
import jax.numpy as jnp
from jax import lax

P_SIZE = 256
EIG = 16
DET = 32
RAD = 13
NR = 512
NC = 1024


def draw_pixels(key, part):
    order = jax.random.permutation(key, DET * DET).astype(jnp.int32)
    positions = jnp.arange(DET * DET, dtype=jnp.int32)
    det_x = positions % DET - DET // 2
    det_y = positions // DET - DET // 2
    inside = (det_x * det_x + det_y * det_y <= RAD * RAD).astype(jnp.int32)
    scores = inside * (DET * DET) + order
    _, chosen = lax.top_k(scores, P_SIZE)
    return chosen.astype(jnp.int32)


def block_scale(key, extent, cuts, smallest, high):
    level = 1.0
    for axis_at, blocks in cuts:
        draws = jax.random.uniform(jax.random.fold_in(jax.random.fold_in(key, 6), axis_at), (blocks,), jnp.float32, smallest / len(cuts), high / len(cuts))
        level = level * jnp.repeat(jnp.exp(draws), extent[axis_at] // blocks).reshape((-1,) + (1,) * (len(extent) - 1 - axis_at))
    return level


def gaussian(key, dims, deviation, bound, kind=jnp.bfloat16):
    result = jax.random.normal(key, dims, jnp.float32) * deviation
    return jnp.minimum(jnp.maximum(result, -bound), bound).astype(kind)


def setup_inputs(seed: int = 0) -> dict:
    keys = jax.random.split(jax.random.key(seed), 5)
    frames = jnp.clip(0.19921875 + 1.5976562 * jax.random.uniform(keys[0], (NR, NC, P_SIZE), jnp.float32) ** block_scale(keys[0], (NR, NC, P_SIZE), ((0, 8), (1, 16)), -0.2, 0.2), 0.19921875, 1.796875).astype(jnp.bfloat16)
    pixel_gain = jnp.clip(1.0 + 0.1 * jax.random.normal(keys[1], (P_SIZE,), jnp.float32), 0.5, 1.5)
    eigen_flats = gaussian(keys[2], (EIG, P_SIZE), P_SIZE ** -0.5, 0.375, jnp.float32)
    pixels = draw_pixels(jax.random.fold_in(keys[4], 71), 0)
    return {"frames": frames, "pixel_gain": pixel_gain, "eigen_flats": eigen_flats, "pixels": pixels}


def flatten(frames, pixel_gain, eigen_flats):
    readings = frames.astype(jnp.float32)
    exposure = jnp.mean(readings, axis=2, keepdims=True)
    scaled = readings * pixel_gain / exposure
    fit_weights = jnp.einsum("rcp,ep->rce", scaled, eigen_flats, precision=lax.Precision.HIGHEST)
    fitted = jnp.einsum("rce,ep->prc", fit_weights, eigen_flats, precision=lax.Precision.HIGHEST)
    return (jnp.transpose(scaled, (2, 0, 1)) - fitted).astype(jnp.bfloat16)


def waves(left_ids, right_ids, length):
    product = (left_ids[:, None] * right_ids[None, :]) % length
    phases = product.astype(jnp.float32) * (2.0 * math.pi / length)
    return jnp.cos(phases), jnp.sin(phases)


def sideband(row_freq, col_freq, chosen, row_count, col_count):
    signed_row = jnp.where(row_freq >= row_count // 2, row_freq - row_count, row_freq)
    signed_col = jnp.where(col_freq >= col_count // 2, col_freq - col_count, col_freq)
    shift_row = (signed_row * (4 * RAD)) // row_count
    shift_col = (signed_col * (4 * RAD)) // col_count
    det_x = (chosen % DET - DET // 2)[:, None, None]
    det_y = (chosen // DET - DET // 2)[:, None, None]
    move_x = shift_row[None, :, None]
    move_y = shift_col[None, None, :]
    upper_disk = (det_x - move_x) * (det_x - move_x) + (det_y - move_y) * (det_y - move_y) <= RAD * RAD
    lower_disk = (det_x + move_x) * (det_x + move_x) + (det_y + move_y) * (det_y + move_y) <= RAD * RAD
    return upper_disk.astype(jnp.float32) - lower_disk.astype(jnp.float32)


def reference(frames, pixel_gain, eigen_flats, pixels):
    highest = lax.Precision.HIGHEST
    flattened = flatten(frames, pixel_gain, eigen_flats)
    row_ids = jnp.arange(NR, dtype=jnp.int32)
    col_ids = jnp.arange(NC, dtype=jnp.int32)
    inverse_rowcos, inverse_rowsin = waves(row_ids, row_ids, NR)
    inverse_colcos, inverse_colsin = waves(col_ids, col_ids, NC)
    forward_rowcos = inverse_rowcos.astype(jnp.bfloat16).astype(jnp.float32)
    forward_rowsin = inverse_rowsin.astype(jnp.bfloat16).astype(jnp.float32)
    forward_colcos = inverse_colcos.astype(jnp.bfloat16).astype(jnp.float32)
    forward_colsin = inverse_colsin.astype(jnp.bfloat16).astype(jnp.float32)
    groups = flattened.reshape(P_SIZE // 16, 16, NR, NC)
    pix_groups = pixels.reshape(P_SIZE // 16, 16)

    def accumulate(totals, pieces):
        pixel_block, chosen = pieces
        values = pixel_block.astype(jnp.float32)
        real_part = jnp.einsum("kr,prc->pkc", forward_rowcos, values, precision=highest).astype(jnp.bfloat16)
        imag_part = (-jnp.einsum("kr,prc->pkc", forward_rowsin, values, precision=highest)).astype(jnp.bfloat16)
        real_part = lax.optimization_barrier(real_part).astype(jnp.float32)
        imag_part = lax.optimization_barrier(imag_part).astype(jnp.float32)
        grid_real = (jnp.einsum("pkc,jc->pkj", real_part, forward_colcos, precision=highest)
                     + jnp.einsum("pkc,jc->pkj", imag_part, forward_colsin, precision=highest))
        grid_imag = (jnp.einsum("pkc,jc->pkj", imag_part, forward_colcos, precision=highest)
                     - jnp.einsum("pkc,jc->pkj", real_part, forward_colsin, precision=highest))
        sideband_weight = sideband(row_ids, col_ids, chosen, NR, NC)
        new_real = totals[0] + jnp.sum(sideband_weight * grid_real, axis=0)
        new_imag = totals[1] + jnp.sum(sideband_weight * grid_imag, axis=0)
        return (new_real, new_imag), None

    start = (jnp.zeros((NR, NC), jnp.float32), jnp.zeros((NR, NC), jnp.float32))
    (psi_real, psi_imag), _ = lax.scan(accumulate, start, (groups, pix_groups))
    half_real = (jnp.dot(psi_real, inverse_colcos, precision=highest, preferred_element_type=jnp.float32)
                 - jnp.dot(psi_imag, inverse_colsin, precision=highest, preferred_element_type=jnp.float32))
    half_imag = (jnp.dot(psi_real, inverse_colsin, precision=highest, preferred_element_type=jnp.float32)
                 + jnp.dot(psi_imag, inverse_colcos, precision=highest, preferred_element_type=jnp.float32))
    out_real = (jnp.dot(inverse_rowcos, half_real, precision=highest, preferred_element_type=jnp.float32)
                - jnp.dot(inverse_rowsin, half_imag, precision=highest, preferred_element_type=jnp.float32))
    out_imag = (jnp.dot(inverse_rowsin, half_real, precision=highest, preferred_element_type=jnp.float32)
                + jnp.dot(inverse_rowcos, half_imag, precision=highest, preferred_element_type=jnp.float32))
    inverse_scale = 1.0 / (NR * NC)
    return jnp.stack([out_real, out_imag], axis=1) * inverse_scale
```

```python
import math

import jax
import jax.numpy as jnp
from jax import lax
from jax.sharding import PartitionSpec as P

DET = 32
RAD = 13
HIGHEST = lax.Precision.HIGHEST


def waves(left_ids, right_ids, length):
    product = left_ids[:, None] * right_ids[None, :] % length
    phases = product.astype(jnp.float32) * (2.0 * math.pi / length)
    return (jnp.cos(phases), jnp.sin(phases))


def shift_index(freq, count):
    signed = jnp.where(freq >= count // 2, freq - count, freq)
    return signed * (4 * RAD) // count + 2 * RAD


def split_dot(left, right):
    hi = left.astype(jnp.bfloat16)
    lo = (left - hi.astype(jnp.float32)).astype(jnp.bfloat16)
    return jnp.dot(hi, right, preferred_element_type=jnp.float32) + jnp.dot(
        lo, right, preferred_element_type=jnp.float32
    )


def on_device(frames, pixel_gain, eigen_flats, pixels):
    n_srow = lax.axis_size("srow")
    n_scol = lax.axis_size("scol")
    n_dev = n_srow * n_scol
    local_rows, local_cols, n_pix = frames.shape
    row_count = local_rows * n_srow
    col_count = local_cols * n_scol
    n_shift = 4 * RAD
    flat_index = lax.axis_index("scol") * n_srow + lax.axis_index("srow")

    readings = frames.astype(jnp.float32)
    exposure = jnp.mean(readings, axis=2, keepdims=True)
    scaled = readings * pixel_gain / exposure
    fit_weights = jnp.einsum("rcp,ep->rce", scaled, eigen_flats, precision=HIGHEST)
    fitted = jnp.einsum("rce,ep->rcp", fit_weights, eigen_flats, precision=HIGHEST)
    flattened = (scaled - fitted).astype(jnp.bfloat16)

    gathered = lax.all_to_all(flattened, "srow", split_axis=1, concat_axis=0, tiled=True)
    cols_here = gathered.shape[1]

    row_ids = jnp.arange(row_count, dtype=jnp.int32)
    row_cos, row_sin = waves(row_ids, row_ids, row_count)
    forward_rows = jnp.concatenate([row_cos, -row_sin], axis=0).astype(jnp.bfloat16)
    spec = jnp.dot(
        forward_rows, gathered.reshape(row_count, cols_here * n_pix), preferred_element_type=jnp.float32
    ).astype(jnp.bfloat16)
    spec = spec.reshape(2, row_count, cols_here, n_pix).transpose(1, 0, 2, 3)
    spec = spec.reshape(row_count, 2 * cols_here, n_pix)

    det_x = (pixels % DET - DET // 2)[None, None, :]
    det_y = (pixels // DET - DET // 2)[None, None, :]
    move_x = (shift_index(row_ids, row_count) - 2 * RAD)[:, None, None]
    move_y = (jnp.arange(n_shift, dtype=jnp.int32) - 2 * RAD)[None, :, None]
    upper = (det_x - move_x) * (det_x - move_x) + (det_y - move_y) * (det_y - move_y) <= RAD * RAD
    lower = (det_x + move_x) * (det_x + move_x) + (det_y + move_y) * (det_y + move_y) <= RAD * RAD
    weight = (upper.astype(jnp.float32) - lower.astype(jnp.float32)).astype(jnp.bfloat16)
    summed = jnp.einsum("kyp,kcp->kyc", weight, spec, preferred_element_type=jnp.float32)
    summed = summed.reshape(row_count, n_shift, 2, cols_here)

    summed = lax.all_to_all(summed, ("scol", "srow"), split_axis=0, concat_axis=3, tiled=True)
    k_here = summed.shape[0]

    col_ids = jnp.arange(col_count, dtype=jnp.int32)
    col_cos, col_sin = waves(col_ids, col_ids, col_count)
    forward_cols = jnp.concatenate(
        [
            jnp.concatenate([col_cos, -col_sin], axis=1),
            jnp.concatenate([col_sin, col_cos], axis=1),
        ],
        axis=0,
    ).astype(jnp.bfloat16)
    per_shift = split_dot(summed.reshape(k_here * n_shift, 2 * col_count), forward_cols)
    per_shift = per_shift.reshape(k_here, n_shift, 2, col_count)
    pick = shift_index(col_ids, col_count)[None, :] == jnp.arange(n_shift, dtype=jnp.int32)[:, None]
    psi = jnp.sum(jnp.where(pick[None, :, None, :], per_shift, 0.0), axis=1)

    psi = lax.all_to_all(psi, ("scol", "srow"), split_axis=2, concat_axis=0, tiled=True)
    j_here = psi.shape[2]
    inverse_rows = jnp.concatenate(
        [
            jnp.concatenate([row_cos, -row_sin], axis=1),
            jnp.concatenate([row_sin, row_cos], axis=1),
        ],
        axis=0,
    )
    psi = psi.transpose(1, 0, 2).reshape(2 * row_count, j_here)
    half = jnp.dot(inverse_rows, psi, precision=HIGHEST, preferred_element_type=jnp.float32)
    half = half.reshape(2, row_count, j_here)

    half = lax.all_to_all(half, "scol", split_axis=1, concat_axis=2, tiled=True)
    half = lax.all_gather(half, "srow", axis=2, tiled=True)
    out_rows = half.shape[1]
    out_cols = col_count // n_srow
    place = jnp.arange(col_count, dtype=jnp.int32)
    j_order = (
        ((place // j_here) % n_scol) * (n_srow * j_here)
        + (place // (j_here * n_scol)) * j_here
        + place % j_here
    )
    my_cols = lax.axis_index("srow") * out_cols + jnp.arange(out_cols, dtype=jnp.int32)
    inv_cos, inv_sin = waves(j_order, my_cols, col_count)
    inverse_cols = jnp.concatenate(
        [
            jnp.concatenate([inv_cos, inv_sin], axis=1),
            jnp.concatenate([-inv_sin, inv_cos], axis=1),
        ],
        axis=0,
    )
    half = half.transpose(1, 0, 2).reshape(out_rows, 2 * col_count)
    image = jnp.dot(half, inverse_cols, precision=HIGHEST, preferred_element_type=jnp.float32)
    image = image * (1.0 / (row_count * col_count))
    return image.reshape(out_rows, 2, out_cols)


def solution(mesh):
    placed = (P("srow", "scol", None), P(), P(), P())
    return jax.shard_map(
        on_device, mesh=mesh, in_specs=placed, out_specs=P("scol", None, "srow"), check_vma=False
    )
```

```python
import math

import jax
import jax.numpy as jnp
from jax import lax
from jax.sharding import PartitionSpec as P

DET = 32
RAD = 13
HIGHEST = lax.Precision.HIGHEST


def waves(left_ids, right_ids, length):
    product = left_ids[:, None] * right_ids[None, :] % length
    phases = product.astype(jnp.float32) * (2.0 * math.pi / length)
    return (jnp.cos(phases), jnp.sin(phases))


def square_waves(count):
    minor = min(128, count)
    ids = jnp.arange(count, dtype=jnp.int32)
    major_cos, major_sin = waves(ids, jnp.arange(count // minor, dtype=jnp.int32) * minor, count)
    minor_cos, minor_sin = waves(ids, jnp.arange(minor, dtype=jnp.int32), count)
    major_cos = jnp.repeat(major_cos, minor, axis=1)
    major_sin = jnp.repeat(major_sin, minor, axis=1)
    minor_cos = jnp.tile(minor_cos, (1, count // minor))
    minor_sin = jnp.tile(minor_sin, (1, count // minor))
    return (
        major_cos * minor_cos - major_sin * minor_sin,
        major_sin * minor_cos + major_cos * minor_sin,
    )


def shift_index(freq, count):
    signed = jnp.where(freq >= count // 2, freq - count, freq)
    return signed * (4 * RAD) // count + 2 * RAD


def split_dot(left, right):
    hi = lax.reduce_precision(left, exponent_bits=8, mantissa_bits=7)
    lo = left - hi
    return jnp.dot(hi.astype(jnp.bfloat16), right, preferred_element_type=jnp.float32) + jnp.dot(
        lo.astype(jnp.bfloat16), right, preferred_element_type=jnp.float32
    )


def on_device(frames, pixel_gain, eigen_flats, pixels):
    n_srow = lax.axis_size("srow")
    n_scol = lax.axis_size("scol")
    n_dev = n_srow * n_scol
    local_rows, local_cols, n_pix = frames.shape
    row_count = local_rows * n_srow
    col_count = local_cols * n_scol
    n_shift = 4 * RAD
    flat_index = lax.axis_index("scol") * n_srow + lax.axis_index("srow")

    readings = frames.astype(jnp.float32)
    exposure = jnp.mean(readings, axis=2, keepdims=True)
    scaled = readings * pixel_gain / exposure
    fit_weights = jnp.einsum("rcp,ep->rce", scaled, eigen_flats, precision=HIGHEST)
    fitted = jnp.einsum("rce,ep->rcp", fit_weights, eigen_flats, precision=HIGHEST)
    flattened = (scaled - fitted).astype(jnp.bfloat16)

    gathered = lax.all_to_all(flattened, "srow", split_axis=1, concat_axis=0, tiled=True)
    cols_here = gathered.shape[1]

    row_ids = jnp.arange(row_count, dtype=jnp.int32)
    row_cos, row_sin = square_waves(row_count)
    forward_rows = jnp.concatenate([row_cos, -row_sin], axis=0).astype(jnp.bfloat16)
    spec = jnp.dot(
        forward_rows, gathered.reshape(row_count, cols_here * n_pix), preferred_element_type=jnp.float32
    ).astype(jnp.bfloat16)
    spec = spec.reshape(2, row_count, cols_here, n_pix).transpose(1, 0, 2, 3)
    spec = spec.reshape(row_count, 2 * cols_here, n_pix)

    det_x = (pixels % DET - DET // 2)[None, None, :]
    det_y = (pixels // DET - DET // 2)[None, None, :]
    move_x = (shift_index(row_ids, row_count) - 2 * RAD)[:, None, None]
    move_y = (jnp.arange(n_shift, dtype=jnp.int32) - 2 * RAD)[None, :, None]
    upper = (det_x - move_x) * (det_x - move_x) + (det_y - move_y) * (det_y - move_y) <= RAD * RAD
    lower = (det_x + move_x) * (det_x + move_x) + (det_y + move_y) * (det_y + move_y) <= RAD * RAD
    weight = (upper.astype(jnp.float32) - lower.astype(jnp.float32)).astype(jnp.bfloat16)
    summed = jnp.einsum("kcp,kyp->kcy", spec, weight, preferred_element_type=jnp.float32)
    summed = summed.reshape(n_dev, row_count // n_dev, 2 * cols_here, n_shift)

    summed = lax.all_to_all(summed, ("scol", "srow"), split_axis=0, concat_axis=0, tiled=True)
    k_here = summed.shape[1]

    col_ids = jnp.arange(col_count, dtype=jnp.int32)
    col_cos, col_sin = square_waves(col_count)
    col_cos = col_cos.astype(jnp.bfloat16).reshape(n_dev, cols_here, col_count)
    col_sin = col_sin.astype(jnp.bfloat16).reshape(n_dev, cols_here, col_count)
    forward_cols = jnp.stack(
        [
            jnp.concatenate([col_cos, -col_sin], axis=2),
            jnp.concatenate([col_sin, col_cos], axis=2),
        ],
        axis=1,
    ).reshape(n_dev * 2 * cols_here, 2 * col_count)
    lhs = summed.transpose(1, 3, 0, 2).reshape(k_here * n_shift, n_dev * 2 * cols_here)
    per_shift = split_dot(lhs, forward_cols)
    per_shift = per_shift.reshape(k_here, n_shift, 2, col_count)
    pick = shift_index(col_ids, col_count)[None, :] == jnp.arange(n_shift, dtype=jnp.int32)[:, None]
    psi = jnp.sum(jnp.where(pick[None, :, None, :], per_shift, 0.0), axis=1)

    psi = lax.all_to_all(psi, ("scol", "srow"), split_axis=2, concat_axis=0, tiled=True)
    j_here = psi.shape[2]
    inverse_rows = jnp.concatenate(
        [
            jnp.concatenate([row_cos, -row_sin], axis=1),
            jnp.concatenate([row_sin, row_cos], axis=1),
        ],
        axis=0,
    )
    psi = psi.transpose(1, 0, 2).reshape(2 * row_count, j_here)
    half = jnp.dot(inverse_rows, psi, precision=HIGHEST, preferred_element_type=jnp.float32)
    half = half.reshape(2, row_count, j_here)

    half = lax.all_to_all(half, "scol", split_axis=1, concat_axis=2, tiled=True)
    half = jnp.broadcast_to(half[None], (n_srow,) + half.shape)
    half = lax.all_to_all(half, "srow", split_axis=0, concat_axis=0, tiled=True)
    out_rows = half.shape[2]
    out_cols = col_count // n_srow
    place = jnp.arange(col_count, dtype=jnp.int32)
    j_order = (
        ((place // j_here) % n_scol) * (n_srow * j_here)
        + (place // (j_here * n_scol)) * j_here
        + place % j_here
    )
    my_cols = lax.axis_index("srow") * out_cols + jnp.arange(out_cols, dtype=jnp.int32)
    inv_cos, inv_sin = waves(j_order, my_cols, col_count)
    inverse_cols = jnp.concatenate(
        [
            jnp.concatenate([inv_cos, inv_sin], axis=1),
            jnp.concatenate([-inv_sin, inv_cos], axis=1),
        ],
        axis=0,
    )
    half = half.transpose(2, 1, 0, 3).reshape(out_rows, 2 * col_count)
    image = jnp.dot(half, inverse_cols, precision=HIGHEST, preferred_element_type=jnp.float32)
    image = image * (1.0 / (row_count * col_count))
    return image.reshape(out_rows, 2, out_cols)


def solution(mesh):
    placed = (P("srow", "scol", None), P(), P(), P())
    return jax.shard_map(
        on_device, mesh=mesh, in_specs=placed, out_specs=P("scol", None, "srow"), check_vma=False
    )
```

```python
import math

import jax
import jax.numpy as jnp
from jax import lax
from jax.sharding import PartitionSpec as P

DET = 32
RAD = 13
HIGHEST = lax.Precision.HIGHEST


def waves(left_ids, right_ids, length):
    product = left_ids[:, None] * right_ids[None, :] % length
    phases = product.astype(jnp.float32) * (2.0 * math.pi / length)
    return (jnp.cos(phases), jnp.sin(phases))


def square_waves(count):
    minor = min(128, count)
    ids = jnp.arange(count, dtype=jnp.int32)
    major_cos, major_sin = waves(ids, jnp.arange(count // minor, dtype=jnp.int32) * minor, count)
    minor_cos, minor_sin = waves(ids, jnp.arange(minor, dtype=jnp.int32), count)
    major_cos = jnp.repeat(major_cos, minor, axis=1)
    major_sin = jnp.repeat(major_sin, minor, axis=1)
    minor_cos = jnp.tile(minor_cos, (1, count // minor))
    minor_sin = jnp.tile(minor_sin, (1, count // minor))
    return (
        major_cos * minor_cos - major_sin * minor_sin,
        major_sin * minor_cos + major_cos * minor_sin,
    )


def shift_index(freq, count):
    signed = jnp.where(freq >= count // 2, freq - count, freq)
    return signed * (4 * RAD) // count + 2 * RAD


def split_dot(left, right):
    hi = lax.reduce_precision(left, exponent_bits=8, mantissa_bits=7)
    lo = left - hi
    return jnp.dot(hi.astype(jnp.bfloat16), right, preferred_element_type=jnp.float32) + jnp.dot(
        lo.astype(jnp.bfloat16), right, preferred_element_type=jnp.float32
    )


def on_device(frames, pixel_gain, eigen_flats, pixels):
    n_srow = lax.axis_size("srow")
    n_scol = lax.axis_size("scol")
    n_dev = n_srow * n_scol
    local_rows, local_cols, n_pix = frames.shape
    row_count = local_rows * n_srow
    col_count = local_cols * n_scol
    n_shift = 4 * RAD
    flat_index = lax.axis_index("scol") * n_srow + lax.axis_index("srow")

    readings = frames.astype(jnp.float32)
    exposure = jnp.mean(readings, axis=2, keepdims=True)
    scaled = readings * pixel_gain / exposure
    fit_weights = jnp.einsum("rcp,ep->rce", scaled, eigen_flats, precision=HIGHEST)
    fitted = jnp.einsum("rce,ep->rcp", fit_weights, eigen_flats, precision=HIGHEST)
    flattened = (scaled - fitted).astype(jnp.bfloat16)

    gathered = lax.all_to_all(flattened, "srow", split_axis=1, concat_axis=0, tiled=True)
    cols_here = gathered.shape[1]

    row_ids = jnp.arange(row_count, dtype=jnp.int32)
    row_cos, row_sin = square_waves(row_count)
    forward_rows = jnp.concatenate([row_cos, -row_sin], axis=0).astype(jnp.bfloat16)
    spec = jnp.dot(
        forward_rows, gathered.reshape(row_count, cols_here * n_pix), preferred_element_type=jnp.float32
    ).astype(jnp.bfloat16)
    spec = spec.reshape(2, row_count, cols_here, n_pix).transpose(1, 0, 2, 3)
    spec = spec.reshape(row_count, 2 * cols_here, n_pix)

    det_x = (pixels % DET - DET // 2)[None, None, :]
    det_y = (pixels // DET - DET // 2)[None, None, :]
    move_x = (shift_index(row_ids, row_count) - 2 * RAD)[:, None, None]
    move_y = (jnp.arange(n_shift, dtype=jnp.int32) - 2 * RAD)[None, :, None]
    upper = (det_x - move_x) * (det_x - move_x) + (det_y - move_y) * (det_y - move_y) <= RAD * RAD
    lower = (det_x + move_x) * (det_x + move_x) + (det_y + move_y) * (det_y + move_y) <= RAD * RAD
    weight = (upper.astype(jnp.float32) - lower.astype(jnp.float32)).astype(jnp.bfloat16)
    summed = jnp.einsum("kcp,kyp->kyc", spec, weight, preferred_element_type=jnp.float32)

    k_blk = row_count // n_scol
    j_blk = col_count // n_srow
    starts, stops = [], []
    for b in range(n_srow):
        shifts = [
            ((j - col_count if j >= col_count // 2 else j) * (4 * RAD)) // col_count + 2 * RAD
            for j in range(b * j_blk, (b + 1) * j_blk)
        ]
        starts.append(min(shifts))
        stops.append(max(shifts) + 1)
    n_dyl = max(e - s for s, e in zip(starts, stops))
    padded = max(s + n_dyl for s in starts)
    summed = jnp.pad(summed, ((0, 0), (0, padded - n_shift), (0, 0)))
    summed = jnp.stack([summed[:, s : s + n_dyl] for s in starts], axis=1)
    summed = summed.reshape(n_scol, k_blk, n_srow, n_dyl * 2 * cols_here).transpose(0, 2, 1, 3)
    summed = summed.reshape(n_dev, k_blk, n_dyl * 2 * cols_here)
    summed = lax.all_to_all(summed, ("scol", "srow"), split_axis=0, concat_axis=0, tiled=True)

    a_idx = lax.axis_index("scol")
    b_idx = lax.axis_index("srow")
    col_ids = jnp.arange(col_count, dtype=jnp.int32)
    my_j = b_idx * j_blk + jnp.arange(j_blk, dtype=jnp.int32)
    col_cos, col_sin = waves(col_ids, my_j, col_count)
    col_cos = col_cos.astype(jnp.bfloat16).reshape(n_dev, cols_here, j_blk)
    col_sin = col_sin.astype(jnp.bfloat16).reshape(n_dev, cols_here, j_blk)
    forward_cols = jnp.stack(
        [
            jnp.concatenate([col_cos, -col_sin], axis=2),
            jnp.concatenate([col_sin, col_cos], axis=2),
        ],
        axis=1,
    ).reshape(n_dev * 2 * cols_here, 2 * j_blk)
    lhs = summed.reshape(n_dev, k_blk, n_dyl, 2 * cols_here).transpose(1, 2, 0, 3)
    lhs = lhs.reshape(k_blk * n_dyl, n_dev * 2 * cols_here)
    per_shift = split_dot(lhs, forward_cols).reshape(k_blk, n_dyl, 2, j_blk)
    my_start = jnp.array(starts, dtype=jnp.int32)[b_idx]
    pick = (shift_index(my_j, col_count) - my_start)[None, :] == jnp.arange(n_dyl, dtype=jnp.int32)[:, None]
    psi = jnp.sum(jnp.where(pick[None, :, None, :], per_shift, 0.0), axis=1)

    my_k = a_idx * k_blk + jnp.arange(k_blk, dtype=jnp.int32)
    inv_cos, inv_sin = waves(row_ids, my_k, row_count)
    inverse_rows = jnp.concatenate(
        [
            jnp.concatenate([inv_cos, -inv_sin], axis=1),
            jnp.concatenate([inv_sin, inv_cos], axis=1),
        ],
        axis=0,
    )
    psi = psi.transpose(1, 0, 2).reshape(2 * k_blk, j_blk)
    half = jnp.dot(inverse_rows, psi, precision=HIGHEST, preferred_element_type=jnp.float32)
    half = half.reshape(2, n_scol, row_count // n_scol, j_blk).transpose(1, 0, 2, 3)
    half = lax.all_to_all(half, "scol", split_axis=0, concat_axis=0, tiled=True)
    half = jnp.sum(half, axis=0)
    out_rows = half.shape[1]

    out_cols = col_count // n_srow
    inv_cos, inv_sin = waves(my_j, col_ids, col_count)
    inverse_cols = jnp.concatenate(
        [
            jnp.concatenate([inv_cos, inv_sin], axis=1),
            jnp.concatenate([-inv_sin, inv_cos], axis=1),
        ],
        axis=0,
    )
    half = half.transpose(1, 0, 2).reshape(out_rows, 2 * j_blk)
    image = jnp.dot(half, inverse_cols, precision=HIGHEST, preferred_element_type=jnp.float32)
    image = image.reshape(out_rows, 2, n_srow, out_cols).transpose(2, 0, 1, 3)
    image = lax.all_to_all(image, "srow", split_axis=0, concat_axis=0, tiled=True)
    image = jnp.sum(image, axis=0) * (1.0 / (row_count * col_count))
    return image


def solution(mesh):
    placed = (P("srow", "scol", None), P(), P(), P())
    return jax.shard_map(
        on_device, mesh=mesh, in_specs=placed, out_specs=P("scol", None, "srow"), check_vma=False
    )
```

```python
import math

import jax
import jax.numpy as jnp
from jax import lax
from jax.sharding import PartitionSpec as P

DET = 32
RAD = 13
HIGHEST = lax.Precision.HIGHEST


def waves(left_ids, right_ids, length):
    product = left_ids[:, None] * right_ids[None, :] % length
    phases = product.astype(jnp.float32) * (2.0 * math.pi / length)
    return (jnp.cos(phases), jnp.sin(phases))


def square_waves(count):
    minor = min(128, count)
    ids = jnp.arange(count, dtype=jnp.int32)
    major_cos, major_sin = waves(ids, jnp.arange(count // minor, dtype=jnp.int32) * minor, count)
    minor_cos, minor_sin = waves(ids, jnp.arange(minor, dtype=jnp.int32), count)
    major_cos = jnp.repeat(major_cos, minor, axis=1)
    major_sin = jnp.repeat(major_sin, minor, axis=1)
    minor_cos = jnp.tile(minor_cos, (1, count // minor))
    minor_sin = jnp.tile(minor_sin, (1, count // minor))
    return (
        major_cos * minor_cos - major_sin * minor_sin,
        major_sin * minor_cos + major_cos * minor_sin,
    )


def shift_index(freq, count):
    signed = jnp.where(freq >= count // 2, freq - count, freq)
    return signed * (4 * RAD) // count + 2 * RAD


def split_dot(left, right):
    hi = lax.reduce_precision(left, exponent_bits=8, mantissa_bits=7)
    lo = left - hi
    return jnp.dot(hi.astype(jnp.bfloat16), right, preferred_element_type=jnp.float32) + jnp.dot(
        lo.astype(jnp.bfloat16), right, preferred_element_type=jnp.float32
    )


def on_device(frames, pixel_gain, eigen_flats, pixels):
    n_srow = lax.axis_size("srow")
    n_scol = lax.axis_size("scol")
    n_dev = n_srow * n_scol
    local_rows, local_cols, n_pix = frames.shape
    row_count = local_rows * n_srow
    col_count = local_cols * n_scol
    n_shift = 4 * RAD
    flat_index = lax.axis_index("scol") * n_srow + lax.axis_index("srow")

    readings = frames.astype(jnp.float32)
    exposure = jnp.mean(readings, axis=2, keepdims=True)
    scaled = readings * pixel_gain / exposure
    fit_weights = jnp.einsum("rcp,ep->rce", scaled, eigen_flats, precision=HIGHEST)
    fitted = jnp.einsum("rce,ep->rcp", fit_weights, eigen_flats, precision=HIGHEST)
    flattened = (scaled - fitted).astype(jnp.bfloat16)

    gathered = lax.all_to_all(flattened, "srow", split_axis=1, concat_axis=0, tiled=True)
    cols_here = gathered.shape[1]

    k_blk = row_count // n_scol
    j_blk = col_count // n_srow
    row_ids = jnp.arange(row_count, dtype=jnp.int32)
    row_cos, row_sin = square_waves(row_count)
    forward_rows = jnp.stack([row_cos, -row_sin], axis=0).reshape(2, n_scol, k_blk, row_count)
    forward_rows = forward_rows.transpose(1, 0, 2, 3).reshape(2 * row_count, row_count)
    spec = jnp.dot(
        forward_rows.astype(jnp.bfloat16),
        gathered.reshape(row_count, cols_here * n_pix),
        preferred_element_type=jnp.float32,
    ).astype(jnp.bfloat16)
    spec = spec.reshape(n_scol, 2, k_blk, cols_here, n_pix)

    def shift_of(freq, count):
        signed = freq - count if freq >= count // 2 else freq
        return (signed * (4 * RAD)) // count

    dx_first, dy_first = [], []
    for a in range(n_scol):
        shifts = [shift_of(k, row_count) for k in range(a * k_blk, (a + 1) * k_blk)]
        dx_first.append(min(shifts))
    n_dx = max(
        max(shift_of(k, row_count) for k in range(a * k_blk, (a + 1) * k_blk)) - dx_first[a] + 1
        for a in range(n_scol)
    )
    for b in range(n_srow):
        dy_first.append(min(shift_of(j, col_count) for j in range(b * j_blk, (b + 1) * j_blk)))
    n_dyl = max(
        max(shift_of(j, col_count) for j in range(b * j_blk, (b + 1) * j_blk)) - dy_first[b] + 1
        for b in range(n_srow)
    )
    move_x = (jnp.array(dx_first, dtype=jnp.int32)[:, None] + jnp.arange(n_dx, dtype=jnp.int32)[None, :])
    move_y = (jnp.array(dy_first, dtype=jnp.int32)[:, None] + jnp.arange(n_dyl, dtype=jnp.int32)[None, :])
    move_x = move_x[:, None, None, :, None]
    move_y = move_y[None, :, :, None, None]
    det_x = (pixels % DET - DET // 2)[None, None, None, None, :]
    det_y = (pixels // DET - DET // 2)[None, None, None, None, :]
    upper = (det_x - move_x) * (det_x - move_x) + (det_y - move_y) * (det_y - move_y) <= RAD * RAD
    lower = (det_x + move_x) * (det_x + move_x) + (det_y + move_y) * (det_y + move_y) <= RAD * RAD
    weight = (upper.astype(jnp.float32) - lower.astype(jnp.float32)).astype(jnp.bfloat16)
    weight = weight.reshape(n_scol, n_srow * n_dyl * n_dx, n_pix)
    summed = jnp.einsum("axp,arkcp->axcrk", weight, spec, preferred_element_type=jnp.float32)
    summed = summed.reshape(n_scol, n_srow, n_dyl, n_dx, cols_here, 2, k_blk)
    own_dx = (shift_index(row_ids, row_count) - 2 * RAD).reshape(n_scol, k_blk)
    own_dx = own_dx - jnp.array(dx_first, dtype=jnp.int32)[:, None]
    dx_pick = own_dx[:, None, :] == jnp.arange(n_dx, dtype=jnp.int32)[None, :, None]
    dx_pick = dx_pick[:, None, None, :, None, None, :]
    summed = jnp.sum(jnp.where(dx_pick, summed, 0.0), axis=3)
    summed = summed.reshape(n_dev, n_dyl * cols_here * 2 * k_blk)

    summed = lax.all_to_all(summed, ("scol", "srow"), split_axis=0, concat_axis=0, tiled=True)

    a_idx = lax.axis_index("scol")
    b_idx = lax.axis_index("srow")
    col_ids = jnp.arange(col_count, dtype=jnp.int32)
    my_j = b_idx * j_blk + jnp.arange(j_blk, dtype=jnp.int32)
    src_cos, src_sin = waves(jnp.arange(n_dev, dtype=jnp.int32) * cols_here, my_j, col_count)
    by_source = jnp.dot(
        summed.T,
        jnp.concatenate([src_cos, src_sin], axis=1),
        precision=HIGHEST,
        preferred_element_type=jnp.float32,
    ).reshape(n_dyl, cols_here, 2, k_blk, 2, j_blk)
    part_re = by_source[:, :, 0, :, 0] + by_source[:, :, 1, :, 1]
    part_im = by_source[:, :, 1, :, 0] - by_source[:, :, 0, :, 1]
    tw_cos, tw_sin = waves(jnp.arange(cols_here, dtype=jnp.int32), my_j, col_count)
    tw_cos = tw_cos[None, :, None, :]
    tw_sin = tw_sin[None, :, None, :]
    per_shift_re = jnp.sum(part_re * tw_cos + part_im * tw_sin, axis=1)
    per_shift_im = jnp.sum(part_im * tw_cos - part_re * tw_sin, axis=1)
    my_start = jnp.array(dy_first, dtype=jnp.int32)[b_idx]
    pick = (shift_index(my_j, col_count) - 2 * RAD - my_start)[None, :] == jnp.arange(n_dyl, dtype=jnp.int32)[:, None]
    pick = pick[:, None, :]
    psi = jnp.stack(
        [
            jnp.sum(jnp.where(pick, per_shift_re, 0.0), axis=0),
            jnp.sum(jnp.where(pick, per_shift_im, 0.0), axis=0),
        ],
        axis=1,
    )

    my_k = a_idx * k_blk + jnp.arange(k_blk, dtype=jnp.int32)
    inv_cos, inv_sin = waves(row_ids, my_k, row_count)
    inverse_rows = jnp.concatenate(
        [
            jnp.concatenate([inv_cos, -inv_sin], axis=1),
            jnp.concatenate([inv_sin, inv_cos], axis=1),
        ],
        axis=0,
    )
    psi = psi.transpose(1, 0, 2).reshape(2 * k_blk, j_blk)
    half = jnp.dot(inverse_rows, psi, precision=HIGHEST, preferred_element_type=jnp.float32)
    half = half.reshape(2, n_scol, row_count // n_scol, j_blk).transpose(1, 0, 2, 3)
    half = lax.all_to_all(half, "scol", split_axis=0, concat_axis=0, tiled=True)
    half = jnp.sum(half, axis=0)
    out_rows = half.shape[1]

    out_cols = col_count // n_srow
    inv_cos, inv_sin = waves(my_j, col_ids, col_count)
    inverse_cols = jnp.concatenate(
        [
            jnp.concatenate([inv_cos, inv_sin], axis=1),
            jnp.concatenate([-inv_sin, inv_cos], axis=1),
        ],
        axis=0,
    )
    half = half.transpose(1, 0, 2).reshape(out_rows, 2 * j_blk)
    image = jnp.dot(half, inverse_cols, precision=HIGHEST, preferred_element_type=jnp.float32)
    image = image.reshape(out_rows, 2, n_srow, out_cols).transpose(2, 0, 1, 3)
    image = lax.all_to_all(image, "srow", split_axis=0, concat_axis=0, tiled=True)
    image = jnp.sum(image, axis=0) * (1.0 / (row_count * col_count))
    return image


def solution(mesh):
    placed = (P("srow", "scol", None), P(), P(), P())
    return jax.shard_map(
        on_device, mesh=mesh, in_specs=placed, out_specs=P("scol", None, "srow"), check_vma=False
    )
```

```python
import math

import jax
import jax.numpy as jnp
from jax import lax
from jax.sharding import PartitionSpec as P

DET = 32
RAD = 13
HIGHEST = lax.Precision.HIGHEST


def waves(left_ids, right_ids, length):
    product = left_ids[:, None] * right_ids[None, :] % length
    phases = product.astype(jnp.float32) * (2.0 * math.pi / length)
    return (jnp.cos(phases), jnp.sin(phases))


def square_waves(count):
    minor = min(128, count)
    ids = jnp.arange(count, dtype=jnp.int32)
    major_cos, major_sin = waves(ids, jnp.arange(count // minor, dtype=jnp.int32) * minor, count)
    minor_cos, minor_sin = waves(ids, jnp.arange(minor, dtype=jnp.int32), count)
    major_cos = jnp.repeat(major_cos, minor, axis=1)
    major_sin = jnp.repeat(major_sin, minor, axis=1)
    minor_cos = jnp.tile(minor_cos, (1, count // minor))
    minor_sin = jnp.tile(minor_sin, (1, count // minor))
    return (
        major_cos * minor_cos - major_sin * minor_sin,
        major_sin * minor_cos + major_cos * minor_sin,
    )


def shift_index(freq, count):
    signed = jnp.where(freq >= count // 2, freq - count, freq)
    return signed * (4 * RAD) // count + 2 * RAD


def split_dot(left, right):
    hi = lax.reduce_precision(left, exponent_bits=8, mantissa_bits=7)
    lo = left - hi
    return jnp.dot(hi.astype(jnp.bfloat16), right, preferred_element_type=jnp.float32) + jnp.dot(
        lo.astype(jnp.bfloat16), right, preferred_element_type=jnp.float32
    )


def on_device(frames, pixel_gain, eigen_flats, pixels):
    n_srow = lax.axis_size("srow")
    n_scol = lax.axis_size("scol")
    n_dev = n_srow * n_scol
    local_rows, local_cols, n_pix = frames.shape
    row_count = local_rows * n_srow
    col_count = local_cols * n_scol
    n_shift = 4 * RAD
    flat_index = lax.axis_index("scol") * n_srow + lax.axis_index("srow")

    readings = frames.astype(jnp.float32)
    exposure = jnp.mean(readings, axis=2, keepdims=True)
    scaled = readings * pixel_gain / exposure
    fit_weights = jnp.einsum("rcp,ep->rce", scaled, eigen_flats, precision=HIGHEST)
    fitted = jnp.einsum("rce,ep->rcp", fit_weights, eigen_flats, precision=HIGHEST)
    flattened = (scaled - fitted).astype(jnp.bfloat16)

    gathered = lax.all_to_all(flattened, "srow", split_axis=1, concat_axis=0, tiled=True)
    cols_here = gathered.shape[1]

    k_blk = row_count // n_scol
    j_blk = col_count // n_srow
    row_ids = jnp.arange(row_count, dtype=jnp.int32)
    row_cos, row_sin = square_waves(row_count)
    forward_rows = jnp.stack([row_cos, -row_sin], axis=0).reshape(2, n_scol, k_blk, row_count)
    forward_rows = forward_rows.transpose(1, 0, 2, 3).reshape(2 * row_count, row_count)
    spec = jnp.dot(
        forward_rows.astype(jnp.bfloat16),
        gathered.reshape(row_count, cols_here * n_pix),
        preferred_element_type=jnp.float32,
    ).astype(jnp.bfloat16)
    spec = spec.reshape(n_scol, 2 * k_blk * cols_here, n_pix)

    def shift_of(freq, count):
        signed = freq - count if freq >= count // 2 else freq
        return (signed * (4 * RAD)) // count

    dx_first, dy_first = [], []
    for a in range(n_scol):
        shifts = [shift_of(k, row_count) for k in range(a * k_blk, (a + 1) * k_blk)]
        dx_first.append(min(shifts))
    n_dx = max(
        max(shift_of(k, row_count) for k in range(a * k_blk, (a + 1) * k_blk)) - dx_first[a] + 1
        for a in range(n_scol)
    )
    for b in range(n_srow):
        dy_first.append(min(shift_of(j, col_count) for j in range(b * j_blk, (b + 1) * j_blk)))
    n_dyl = max(
        max(shift_of(j, col_count) for j in range(b * j_blk, (b + 1) * j_blk)) - dy_first[b] + 1
        for b in range(n_srow)
    )
    n_dyl = -(-n_dyl // 8) * 8
    move_x = (jnp.array(dx_first, dtype=jnp.int32)[:, None] + jnp.arange(n_dx, dtype=jnp.int32)[None, :])
    move_y = (jnp.array(dy_first, dtype=jnp.int32)[:, None] + jnp.arange(n_dyl, dtype=jnp.int32)[None, :])
    move_x = move_x[:, None, None, :, None]
    move_y = move_y[None, :, :, None, None]
    det_x = (pixels % DET - DET // 2)[None, None, None, None, :]
    det_y = (pixels // DET - DET // 2)[None, None, None, None, :]
    upper = (det_x - move_x) * (det_x - move_x) + (det_y - move_y) * (det_y - move_y) <= RAD * RAD
    lower = (det_x + move_x) * (det_x + move_x) + (det_y + move_y) * (det_y + move_y) <= RAD * RAD
    weight = (upper.astype(jnp.float32) - lower.astype(jnp.float32)).astype(jnp.bfloat16)
    own_dx = (shift_index(row_ids, row_count) - 2 * RAD).reshape(n_scol, k_blk)
    own_dx = own_dx - jnp.array(dx_first, dtype=jnp.int32)[:, None]
    dx_of_n = jnp.broadcast_to(own_dx[:, None, :, None], (n_scol, 2, k_blk, cols_here))
    dx_of_n = dx_of_n.reshape(n_scol, 1, 2 * k_blk * cols_here)
    summed = None
    for d in range(n_dx):
        part = jnp.einsum(
            "axp,anp->axn",
            weight[:, :, :, d].reshape(n_scol, n_srow * n_dyl, n_pix),
            spec,
            preferred_element_type=jnp.float32,
        )
        part = jnp.where(dx_of_n == d, part, 0.0)
        summed = part if summed is None else summed + part
    summed = summed.reshape(n_dev, n_dyl, 2 * k_blk * cols_here)

    summed = lax.all_to_all(summed, ("scol", "srow"), split_axis=0, concat_axis=0, tiled=True)

    a_idx = lax.axis_index("scol")
    b_idx = lax.axis_index("srow")
    col_ids = jnp.arange(col_count, dtype=jnp.int32)
    my_j = b_idx * j_blk + jnp.arange(j_blk, dtype=jnp.int32)
    src_cos, src_sin = waves(jnp.arange(n_dev, dtype=jnp.int32) * cols_here, my_j, col_count)
    by_source = jnp.dot(
        summed.reshape(n_dev, -1).T,
        jnp.concatenate([src_cos, src_sin], axis=1),
        precision=HIGHEST,
        preferred_element_type=jnp.float32,
    ).reshape(n_dyl, 2, k_blk, cols_here, 2, j_blk)
    part_re = by_source[:, 0, :, :, 0] + by_source[:, 1, :, :, 1]
    part_im = by_source[:, 1, :, :, 0] - by_source[:, 0, :, :, 1]
    tw_cos, tw_sin = waves(jnp.arange(cols_here, dtype=jnp.int32), my_j, col_count)
    tw_cos = tw_cos[None, None, :, :]
    tw_sin = tw_sin[None, None, :, :]
    per_shift_re = jnp.sum(part_re * tw_cos + part_im * tw_sin, axis=2)
    per_shift_im = jnp.sum(part_im * tw_cos - part_re * tw_sin, axis=2)
    my_start = jnp.array(dy_first, dtype=jnp.int32)[b_idx]
    pick = (shift_index(my_j, col_count) - 2 * RAD - my_start)[None, :] == jnp.arange(n_dyl, dtype=jnp.int32)[:, None]
    pick = pick[:, None, :]
    psi = jnp.stack(
        [
            jnp.sum(jnp.where(pick, per_shift_re, 0.0), axis=0),
            jnp.sum(jnp.where(pick, per_shift_im, 0.0), axis=0),
        ],
        axis=1,
    )

    my_k = a_idx * k_blk + jnp.arange(k_blk, dtype=jnp.int32)
    inv_cos, inv_sin = waves(row_ids, my_k, row_count)
    inverse_rows = jnp.concatenate(
        [
            jnp.concatenate([inv_cos, -inv_sin], axis=1),
            jnp.concatenate([inv_sin, inv_cos], axis=1),
        ],
        axis=0,
    )
    psi = psi.transpose(1, 0, 2).reshape(2 * k_blk, j_blk)
    half = jnp.dot(inverse_rows, psi, precision=HIGHEST, preferred_element_type=jnp.float32)
    half = half.reshape(2, n_scol, row_count // n_scol, j_blk).transpose(1, 0, 2, 3)
    half = lax.all_to_all(half, "scol", split_axis=0, concat_axis=0, tiled=True)
    half = jnp.sum(half, axis=0)
    out_rows = half.shape[1]

    out_cols = col_count // n_srow
    inv_cos, inv_sin = waves(my_j, col_ids, col_count)
    inverse_cols = jnp.concatenate(
        [
            jnp.concatenate([inv_cos, inv_sin], axis=1),
            jnp.concatenate([-inv_sin, inv_cos], axis=1),
        ],
        axis=0,
    )
    half = half.transpose(1, 0, 2).reshape(out_rows, 2 * j_blk)
    image = jnp.dot(half, inverse_cols, precision=HIGHEST, preferred_element_type=jnp.float32)
    image = image.reshape(out_rows, 2, n_srow, out_cols).transpose(2, 0, 1, 3)
    image = lax.all_to_all(image, "srow", split_axis=0, concat_axis=0, tiled=True)
    image = jnp.sum(image, axis=0) * (1.0 / (row_count * col_count))
    return image


def solution(mesh):
    placed = (P("srow", "scol", None), P(), P(), P())
    return jax.shard_map(
        on_device, mesh=mesh, in_specs=placed, out_specs=P("scol", None, "srow"), check_vma=False
    )
```

```python
import math

import jax
import jax.numpy as jnp
from jax import lax
from jax.sharding import PartitionSpec as P

DET = 32
RAD = 13
HIGHEST = lax.Precision.HIGHEST


def waves(left_ids, right_ids, length):
    product = left_ids[:, None] * right_ids[None, :] % length
    phases = product.astype(jnp.float32) * (2.0 * math.pi / length)
    return (jnp.cos(phases), jnp.sin(phases))


def square_waves(count):
    minor = min(128, count)
    ids = jnp.arange(count, dtype=jnp.int32)
    major_cos, major_sin = waves(ids, jnp.arange(count // minor, dtype=jnp.int32) * minor, count)
    minor_cos, minor_sin = waves(ids, jnp.arange(minor, dtype=jnp.int32), count)
    major_cos = jnp.repeat(major_cos, minor, axis=1)
    major_sin = jnp.repeat(major_sin, minor, axis=1)
    minor_cos = jnp.tile(minor_cos, (1, count // minor))
    minor_sin = jnp.tile(minor_sin, (1, count // minor))
    return (
        major_cos * minor_cos - major_sin * minor_sin,
        major_sin * minor_cos + major_cos * minor_sin,
    )


def shift_index(freq, count):
    signed = jnp.where(freq >= count // 2, freq - count, freq)
    return signed * (4 * RAD) // count + 2 * RAD


def split_dot(left, right):
    hi = lax.reduce_precision(left, exponent_bits=8, mantissa_bits=7)
    lo = left - hi
    return jnp.dot(hi.astype(jnp.bfloat16), right, preferred_element_type=jnp.float32) + jnp.dot(
        lo.astype(jnp.bfloat16), right, preferred_element_type=jnp.float32
    )


def on_device(frames, pixel_gain, eigen_flats, pixels):
    n_srow = lax.axis_size("srow")
    n_scol = lax.axis_size("scol")
    n_dev = n_srow * n_scol
    local_rows, local_cols, n_pix = frames.shape
    row_count = local_rows * n_srow
    col_count = local_cols * n_scol
    n_shift = 4 * RAD
    flat_index = lax.axis_index("scol") * n_srow + lax.axis_index("srow")

    readings = frames.astype(jnp.float32)
    exposure = jnp.mean(readings, axis=2, keepdims=True)
    scaled = readings * pixel_gain / exposure
    fit_weights = jnp.einsum("rcp,ep->rce", scaled, eigen_flats, precision=lax.Precision.HIGH)
    fitted = jnp.einsum("rce,ep->rcp", fit_weights, eigen_flats, precision=lax.Precision.HIGH)
    flattened = (scaled - fitted).astype(jnp.bfloat16)

    gathered = lax.all_to_all(flattened, "srow", split_axis=1, concat_axis=0, tiled=True)
    cols_here = gathered.shape[1]

    k_blk = row_count // n_scol
    j_blk = col_count // n_srow
    row_ids = jnp.arange(row_count, dtype=jnp.int32)
    row_cos, row_sin = square_waves(row_count)
    forward_rows = jnp.stack([row_cos, -row_sin], axis=0).reshape(2, n_scol, k_blk, row_count)
    forward_rows = forward_rows.transpose(1, 0, 2, 3).reshape(2 * row_count, row_count)
    spec = jnp.dot(
        forward_rows.astype(jnp.bfloat16),
        gathered.reshape(row_count, cols_here * n_pix),
        preferred_element_type=jnp.float32,
    ).astype(jnp.bfloat16)
    spec = spec.reshape(n_scol, 2 * k_blk * cols_here, n_pix)

    def shift_of(freq, count):
        signed = freq - count if freq >= count // 2 else freq
        return (signed * (4 * RAD)) // count

    dx_first, dy_first = [], []
    for a in range(n_scol):
        shifts = [shift_of(k, row_count) for k in range(a * k_blk, (a + 1) * k_blk)]
        dx_first.append(min(shifts))
    n_dx = max(
        max(shift_of(k, row_count) for k in range(a * k_blk, (a + 1) * k_blk)) - dx_first[a] + 1
        for a in range(n_scol)
    )
    for b in range(n_srow):
        dy_first.append(min(shift_of(j, col_count) for j in range(b * j_blk, (b + 1) * j_blk)))
    n_dyl = max(
        max(shift_of(j, col_count) for j in range(b * j_blk, (b + 1) * j_blk)) - dy_first[b] + 1
        for b in range(n_srow)
    )
    n_dyl = -(-n_dyl // 8) * 8
    move_x = (jnp.array(dx_first, dtype=jnp.int32)[:, None] + jnp.arange(n_dx, dtype=jnp.int32)[None, :])
    move_y = (jnp.array(dy_first, dtype=jnp.int32)[:, None] + jnp.arange(n_dyl, dtype=jnp.int32)[None, :])
    move_x = move_x[:, None, None, :, None]
    move_y = move_y[None, :, :, None, None]
    det_x = (pixels % DET - DET // 2)[None, None, None, None, :]
    det_y = (pixels // DET - DET // 2)[None, None, None, None, :]
    upper = (det_x - move_x) * (det_x - move_x) + (det_y - move_y) * (det_y - move_y) <= RAD * RAD
    lower = (det_x + move_x) * (det_x + move_x) + (det_y + move_y) * (det_y + move_y) <= RAD * RAD
    weight = (upper.astype(jnp.float32) - lower.astype(jnp.float32)).astype(jnp.bfloat16)
    own_dx = (shift_index(row_ids, row_count) - 2 * RAD).reshape(n_scol, k_blk)
    own_dx = own_dx - jnp.array(dx_first, dtype=jnp.int32)[:, None]
    dx_of_n = jnp.broadcast_to(own_dx[:, None, :, None], (n_scol, 2, k_blk, cols_here))
    dx_of_n = dx_of_n.reshape(n_scol, 1, 2 * k_blk * cols_here)
    summed = None
    for d in range(n_dx):
        part = jnp.einsum(
            "axp,anp->axn",
            weight[:, :, :, d].reshape(n_scol, n_srow * n_dyl, n_pix),
            spec,
            preferred_element_type=jnp.float32,
        )
        part = jnp.where(dx_of_n == d, part, 0.0)
        summed = part if summed is None else summed + part
    summed = summed.reshape(n_dev, n_dyl, 2 * k_blk * cols_here).astype(jnp.bfloat16)

    summed = lax.all_to_all(summed, ("scol", "srow"), split_axis=0, concat_axis=0, tiled=True)

    a_idx = lax.axis_index("scol")
    b_idx = lax.axis_index("srow")
    col_ids = jnp.arange(col_count, dtype=jnp.int32)
    my_j = b_idx * j_blk + jnp.arange(j_blk, dtype=jnp.int32)
    src_cos, src_sin = waves(jnp.arange(n_dev, dtype=jnp.int32) * cols_here, my_j, col_count)
    by_source = jnp.dot(
        summed.reshape(n_dev, -1).T.astype(jnp.float32),
        jnp.concatenate([src_cos, src_sin], axis=1),
        precision=HIGHEST,
        preferred_element_type=jnp.float32,
    ).reshape(n_dyl, 2, k_blk, cols_here, 2, j_blk)
    part_re = by_source[:, 0, :, :, 0] + by_source[:, 1, :, :, 1]
    part_im = by_source[:, 1, :, :, 0] - by_source[:, 0, :, :, 1]
    tw_cos, tw_sin = waves(jnp.arange(cols_here, dtype=jnp.int32), my_j, col_count)
    tw_cos = tw_cos[None, None, :, :]
    tw_sin = tw_sin[None, None, :, :]
    per_shift_re = jnp.sum(part_re * tw_cos + part_im * tw_sin, axis=2)
    per_shift_im = jnp.sum(part_im * tw_cos - part_re * tw_sin, axis=2)
    my_start = jnp.array(dy_first, dtype=jnp.int32)[b_idx]
    pick = (shift_index(my_j, col_count) - 2 * RAD - my_start)[None, :] == jnp.arange(n_dyl, dtype=jnp.int32)[:, None]
    pick = pick[:, None, :]
    psi = jnp.stack(
        [
            jnp.sum(jnp.where(pick, per_shift_re, 0.0), axis=0),
            jnp.sum(jnp.where(pick, per_shift_im, 0.0), axis=0),
        ],
        axis=1,
    )

    my_k = a_idx * k_blk + jnp.arange(k_blk, dtype=jnp.int32)
    inv_cos, inv_sin = waves(row_ids, my_k, row_count)
    inverse_rows = jnp.concatenate(
        [
            jnp.concatenate([inv_cos, -inv_sin], axis=1),
            jnp.concatenate([inv_sin, inv_cos], axis=1),
        ],
        axis=0,
    )
    psi = psi.transpose(1, 0, 2).reshape(2 * k_blk, j_blk)
    half = jnp.dot(inverse_rows, psi, precision=HIGHEST, preferred_element_type=jnp.float32)
    half = half.reshape(2, n_scol, row_count // n_scol, j_blk).transpose(1, 0, 2, 3)
    half = lax.all_to_all(half, "scol", split_axis=0, concat_axis=0, tiled=True)
    half = jnp.sum(half, axis=0)
    out_rows = half.shape[1]

    out_cols = col_count // n_srow
    inv_cos, inv_sin = waves(my_j, col_ids, col_count)
    inverse_cols = jnp.concatenate(
        [
            jnp.concatenate([inv_cos, inv_sin], axis=1),
            jnp.concatenate([-inv_sin, inv_cos], axis=1),
        ],
        axis=0,
    )
    half = half.transpose(1, 0, 2).reshape(out_rows, 2 * j_blk)
    image = jnp.dot(half, inverse_cols, precision=HIGHEST, preferred_element_type=jnp.float32)
    image = image.reshape(out_rows, 2, n_srow, out_cols).transpose(2, 0, 1, 3)
    image = lax.all_to_all(image, "srow", split_axis=0, concat_axis=0, tiled=True)
    image = jnp.sum(image, axis=0) * (1.0 / (row_count * col_count))
    return image


def solution(mesh):
    placed = (P("srow", "scol", None), P(), P(), P())
    return jax.shard_map(
        on_device, mesh=mesh, in_specs=placed, out_specs=P("scol", None, "srow"), check_vma=False
    )
```

```python
import math

import jax
import jax.numpy as jnp
from jax import lax
from jax.sharding import PartitionSpec as P

DET = 32
RAD = 13
HIGHEST = lax.Precision.HIGHEST


def waves(left_ids, right_ids, length):
    product = left_ids[:, None] * right_ids[None, :] % length
    phases = product.astype(jnp.float32) * (2.0 * math.pi / length)
    return (jnp.cos(phases), jnp.sin(phases))


def square_waves(count):
    minor = min(128, count)
    ids = jnp.arange(count, dtype=jnp.int32)
    major_cos, major_sin = waves(ids, jnp.arange(count // minor, dtype=jnp.int32) * minor, count)
    minor_cos, minor_sin = waves(ids, jnp.arange(minor, dtype=jnp.int32), count)
    major_cos = jnp.repeat(major_cos, minor, axis=1)
    major_sin = jnp.repeat(major_sin, minor, axis=1)
    minor_cos = jnp.tile(minor_cos, (1, count // minor))
    minor_sin = jnp.tile(minor_sin, (1, count // minor))
    return (
        major_cos * minor_cos - major_sin * minor_sin,
        major_sin * minor_cos + major_cos * minor_sin,
    )


def shift_index(freq, count):
    signed = jnp.where(freq >= count // 2, freq - count, freq)
    return signed * (4 * RAD) // count + 2 * RAD


def split_dot(left, right):
    hi = lax.reduce_precision(left, exponent_bits=8, mantissa_bits=7)
    lo = left - hi
    return jnp.dot(hi.astype(jnp.bfloat16), right, preferred_element_type=jnp.float32) + jnp.dot(
        lo.astype(jnp.bfloat16), right, preferred_element_type=jnp.float32
    )


def on_device(frames, pixel_gain, eigen_flats, pixels):
    n_srow = lax.axis_size("srow")
    n_scol = lax.axis_size("scol")
    n_dev = n_srow * n_scol
    local_rows, local_cols, n_pix = frames.shape
    row_count = local_rows * n_srow
    col_count = local_cols * n_scol
    n_shift = 4 * RAD
    flat_index = lax.axis_index("scol") * n_srow + lax.axis_index("srow")

    readings = frames.astype(jnp.float32)
    exposure = jnp.mean(readings, axis=2, keepdims=True)
    scaled = readings * pixel_gain / exposure
    fit_weights = jnp.einsum("rcp,ep->rce", scaled, eigen_flats, precision=lax.Precision.HIGH)
    fitted = jnp.einsum("rce,ep->rcp", fit_weights, eigen_flats, precision=lax.Precision.HIGH)
    flattened = (scaled - fitted).astype(jnp.bfloat16)

    n_half = 2
    p_half = n_pix // n_half
    gathered = [
        lax.all_to_all(
            flattened[:, :, h * p_half : (h + 1) * p_half], "srow", split_axis=1, concat_axis=0, tiled=True
        )
        for h in range(n_half)
    ]
    cols_here = gathered[0].shape[1]

    k_blk = row_count // n_scol
    j_blk = col_count // n_srow
    row_ids = jnp.arange(row_count, dtype=jnp.int32)
    row_cos, row_sin = square_waves(row_count)
    forward_rows = jnp.stack([row_cos, -row_sin], axis=0).reshape(2, n_scol, k_blk, row_count)
    forward_rows = forward_rows.transpose(1, 0, 2, 3).reshape(2 * row_count, row_count)
    forward_rows = forward_rows.astype(jnp.bfloat16)

    def shift_of(freq, count):
        signed = freq - count if freq >= count // 2 else freq
        return (signed * (4 * RAD)) // count

    dx_first, dy_first = [], []
    for a in range(n_scol):
        shifts = [shift_of(k, row_count) for k in range(a * k_blk, (a + 1) * k_blk)]
        dx_first.append(min(shifts))
    n_dx = max(
        max(shift_of(k, row_count) for k in range(a * k_blk, (a + 1) * k_blk)) - dx_first[a] + 1
        for a in range(n_scol)
    )
    for b in range(n_srow):
        dy_first.append(min(shift_of(j, col_count) for j in range(b * j_blk, (b + 1) * j_blk)))
    n_dyl = max(
        max(shift_of(j, col_count) for j in range(b * j_blk, (b + 1) * j_blk)) - dy_first[b] + 1
        for b in range(n_srow)
    )
    n_dyl = -(-n_dyl // 8) * 8
    move_x = (jnp.array(dx_first, dtype=jnp.int32)[:, None] + jnp.arange(n_dx, dtype=jnp.int32)[None, :])
    move_y = (jnp.array(dy_first, dtype=jnp.int32)[:, None] + jnp.arange(n_dyl, dtype=jnp.int32)[None, :])
    move_x = move_x[:, None, None, :, None]
    move_y = move_y[None, :, :, None, None]
    det_x = (pixels % DET - DET // 2)[None, None, None, None, :]
    det_y = (pixels // DET - DET // 2)[None, None, None, None, :]
    upper = (det_x - move_x) * (det_x - move_x) + (det_y - move_y) * (det_y - move_y) <= RAD * RAD
    lower = (det_x + move_x) * (det_x + move_x) + (det_y + move_y) * (det_y + move_y) <= RAD * RAD
    weight = (upper.astype(jnp.float32) - lower.astype(jnp.float32)).astype(jnp.bfloat16)
    own_dx = (shift_index(row_ids, row_count) - 2 * RAD).reshape(n_scol, k_blk)
    own_dx = own_dx - jnp.array(dx_first, dtype=jnp.int32)[:, None]
    dx_of_n = jnp.broadcast_to(own_dx[:, None, :, None], (n_scol, 2, k_blk, cols_here))
    dx_of_n = dx_of_n.reshape(n_scol, 1, 2 * k_blk * cols_here)
    summed = None
    for h in range(n_half):
        spec = jnp.dot(
            forward_rows,
            gathered[h].reshape(row_count, cols_here * p_half),
            preferred_element_type=jnp.float32,
        ).astype(jnp.bfloat16)
        spec = spec.reshape(n_scol, 2 * k_blk * cols_here, p_half)
        for d in range(n_dx):
            part = jnp.einsum(
                "axp,anp->axn",
                weight[:, :, :, d, h * p_half : (h + 1) * p_half].reshape(n_scol, n_srow * n_dyl, p_half),
                spec,
                preferred_element_type=jnp.float32,
            )
            part = jnp.where(dx_of_n == d, part, 0.0)
            summed = part if summed is None else summed + part
    summed = summed.reshape(n_dev, n_dyl, 2 * k_blk * cols_here).astype(jnp.bfloat16)

    summed = lax.all_to_all(summed, ("scol", "srow"), split_axis=0, concat_axis=0, tiled=True)

    a_idx = lax.axis_index("scol")
    b_idx = lax.axis_index("srow")
    col_ids = jnp.arange(col_count, dtype=jnp.int32)
    my_j = b_idx * j_blk + jnp.arange(j_blk, dtype=jnp.int32)
    src_cos, src_sin = waves(jnp.arange(n_dev, dtype=jnp.int32) * cols_here, my_j, col_count)
    by_source = jnp.dot(
        summed.reshape(n_dev, -1).T.astype(jnp.float32),
        jnp.concatenate([src_cos, src_sin], axis=1),
        precision=HIGHEST,
        preferred_element_type=jnp.float32,
    ).reshape(n_dyl, 2, k_blk, cols_here, 2, j_blk)
    part_re = by_source[:, 0, :, :, 0] + by_source[:, 1, :, :, 1]
    part_im = by_source[:, 1, :, :, 0] - by_source[:, 0, :, :, 1]
    tw_cos, tw_sin = waves(jnp.arange(cols_here, dtype=jnp.int32), my_j, col_count)
    tw_cos = tw_cos[None, None, :, :]
    tw_sin = tw_sin[None, None, :, :]
    per_shift_re = jnp.sum(part_re * tw_cos + part_im * tw_sin, axis=2)
    per_shift_im = jnp.sum(part_im * tw_cos - part_re * tw_sin, axis=2)
    my_start = jnp.array(dy_first, dtype=jnp.int32)[b_idx]
    pick = (shift_index(my_j, col_count) - 2 * RAD - my_start)[None, :] == jnp.arange(n_dyl, dtype=jnp.int32)[:, None]
    pick = pick[:, None, :]
    psi = jnp.stack(
        [
            jnp.sum(jnp.where(pick, per_shift_re, 0.0), axis=0),
            jnp.sum(jnp.where(pick, per_shift_im, 0.0), axis=0),
        ],
        axis=1,
    )

    my_k = a_idx * k_blk + jnp.arange(k_blk, dtype=jnp.int32)
    inv_cos, inv_sin = waves(row_ids, my_k, row_count)
    inverse_rows = jnp.concatenate(
        [
            jnp.concatenate([inv_cos, -inv_sin], axis=1),
            jnp.concatenate([inv_sin, inv_cos], axis=1),
        ],
        axis=0,
    )
    psi = psi.transpose(1, 0, 2).reshape(2 * k_blk, j_blk)
    half = jnp.dot(inverse_rows, psi, precision=HIGHEST, preferred_element_type=jnp.float32)
    half = half.reshape(2, n_scol, row_count // n_scol, j_blk).transpose(1, 0, 2, 3)
    half = lax.all_to_all(half, "scol", split_axis=0, concat_axis=0, tiled=True)
    half = jnp.sum(half, axis=0)
    out_rows = half.shape[1]

    out_cols = col_count // n_srow
    inv_cos, inv_sin = waves(my_j, col_ids, col_count)
    inverse_cols = jnp.concatenate(
        [
            jnp.concatenate([inv_cos, inv_sin], axis=1),
            jnp.concatenate([-inv_sin, inv_cos], axis=1),
        ],
        axis=0,
    )
    half = half.transpose(1, 0, 2).reshape(out_rows, 2 * j_blk)
    image = jnp.dot(half, inverse_cols, precision=HIGHEST, preferred_element_type=jnp.float32)
    image = image.reshape(out_rows, 2, n_srow, out_cols).transpose(2, 0, 1, 3)
    image = lax.all_to_all(image, "srow", split_axis=0, concat_axis=0, tiled=True)
    image = jnp.sum(image, axis=0) * (1.0 / (row_count * col_count))
    return image


def solution(mesh):
    placed = (P("srow", "scol", None), P(), P(), P())
    return jax.shard_map(
        on_device, mesh=mesh, in_specs=placed, out_specs=P("scol", None, "srow"), check_vma=False
    )
```

```python
import math

import jax
import jax.numpy as jnp
from jax import lax
from jax.sharding import PartitionSpec as P

DET = 32
RAD = 13
HIGHEST = lax.Precision.HIGHEST


def waves(left_ids, right_ids, length):
    product = left_ids[:, None] * right_ids[None, :] % length
    phases = product.astype(jnp.float32) * (2.0 * math.pi / length)
    return (jnp.cos(phases), jnp.sin(phases))


def square_waves(count):
    minor = min(128, count)
    ids = jnp.arange(count, dtype=jnp.int32)
    major_cos, major_sin = waves(ids, jnp.arange(count // minor, dtype=jnp.int32) * minor, count)
    minor_cos, minor_sin = waves(ids, jnp.arange(minor, dtype=jnp.int32), count)
    major_cos = jnp.repeat(major_cos, minor, axis=1)
    major_sin = jnp.repeat(major_sin, minor, axis=1)
    minor_cos = jnp.tile(minor_cos, (1, count // minor))
    minor_sin = jnp.tile(minor_sin, (1, count // minor))
    return (
        major_cos * minor_cos - major_sin * minor_sin,
        major_sin * minor_cos + major_cos * minor_sin,
    )


def shift_index(freq, count):
    signed = jnp.where(freq >= count // 2, freq - count, freq)
    return signed * (4 * RAD) // count + 2 * RAD


def split_dot(left, right):
    hi = lax.reduce_precision(left, exponent_bits=8, mantissa_bits=7)
    lo = left - hi
    return jnp.dot(hi.astype(jnp.bfloat16), right, preferred_element_type=jnp.float32) + jnp.dot(
        lo.astype(jnp.bfloat16), right, preferred_element_type=jnp.float32
    )


def on_device(frames, pixel_gain, eigen_flats, pixels):
    n_srow = lax.axis_size("srow")
    n_scol = lax.axis_size("scol")
    n_dev = n_srow * n_scol
    local_rows, local_cols, n_pix = frames.shape
    row_count = local_rows * n_srow
    col_count = local_cols * n_scol
    n_shift = 4 * RAD
    flat_index = lax.axis_index("scol") * n_srow + lax.axis_index("srow")

    readings = frames.astype(jnp.float32)
    exposure = jnp.mean(readings, axis=2, keepdims=True)
    scaled = readings * pixel_gain / exposure
    fit_weights = jnp.einsum("rcp,ep->rce", scaled, eigen_flats, precision=lax.Precision.HIGH)
    fitted = jnp.einsum("rce,ep->rcp", fit_weights, eigen_flats, precision=lax.Precision.HIGH)
    flattened = (scaled - fitted).astype(jnp.bfloat16)

    gathered = lax.all_to_all(flattened, "srow", split_axis=1, concat_axis=0, tiled=True)
    cols_here = gathered.shape[1]

    k_blk = row_count // n_scol
    j_blk = col_count // n_srow
    row_ids = jnp.arange(row_count, dtype=jnp.int32)
    row_cos, row_sin = square_waves(row_count)
    forward_rows = jnp.stack([row_cos, -row_sin], axis=0).reshape(2, n_scol, k_blk, row_count)
    forward_rows = forward_rows.transpose(1, 0, 2, 3).reshape(2 * row_count, row_count)
    spec = jnp.dot(
        forward_rows.astype(jnp.bfloat16),
        gathered.reshape(row_count, cols_here * n_pix),
        preferred_element_type=jnp.float32,
    ).astype(jnp.bfloat16)
    spec = spec.reshape(n_scol, 2 * k_blk * cols_here, n_pix)

    def shift_of(freq, count):
        signed = freq - count if freq >= count // 2 else freq
        return (signed * (4 * RAD)) // count

    dx_first, dy_first = [], []
    for a in range(n_scol):
        shifts = [shift_of(k, row_count) for k in range(a * k_blk, (a + 1) * k_blk)]
        dx_first.append(min(shifts))
    n_dx = max(
        max(shift_of(k, row_count) for k in range(a * k_blk, (a + 1) * k_blk)) - dx_first[a] + 1
        for a in range(n_scol)
    )
    for b in range(n_srow):
        dy_first.append(min(shift_of(j, col_count) for j in range(b * j_blk, (b + 1) * j_blk)))
    n_dyl = max(
        max(shift_of(j, col_count) for j in range(b * j_blk, (b + 1) * j_blk)) - dy_first[b] + 1
        for b in range(n_srow)
    )
    n_dyl = -(-n_dyl // 8) * 8
    move_x = (jnp.array(dx_first, dtype=jnp.int32)[:, None] + jnp.arange(n_dx, dtype=jnp.int32)[None, :])
    move_y = (jnp.array(dy_first, dtype=jnp.int32)[:, None] + jnp.arange(n_dyl, dtype=jnp.int32)[None, :])
    move_x = move_x[:, None, None, :, None]
    move_y = move_y[None, :, :, None, None]
    det_x = (pixels % DET - DET // 2)[None, None, None, None, :]
    det_y = (pixels // DET - DET // 2)[None, None, None, None, :]
    upper = (det_x - move_x) * (det_x - move_x) + (det_y - move_y) * (det_y - move_y) <= RAD * RAD
    lower = (det_x + move_x) * (det_x + move_x) + (det_y + move_y) * (det_y + move_y) <= RAD * RAD
    weight = (upper.astype(jnp.float32) - lower.astype(jnp.float32)).astype(jnp.bfloat16)
    own_dx = (shift_index(row_ids, row_count) - 2 * RAD).reshape(n_scol, k_blk)
    own_dx = own_dx - jnp.array(dx_first, dtype=jnp.int32)[:, None]
    dx_of_n = jnp.broadcast_to(own_dx[:, None, :, None], (n_scol, 2, k_blk, cols_here))
    dx_of_n = dx_of_n.reshape(n_scol, 1, 2 * k_blk * cols_here)
    summed = None
    for d in range(n_dx):
        part = jnp.einsum(
            "axp,anp->axn",
            weight[:, :, :, d].reshape(n_scol, n_srow * n_dyl, n_pix),
            spec,
            preferred_element_type=jnp.float32,
        )
        part = jnp.where(dx_of_n == d, part, 0.0)
        summed = part if summed is None else summed + part
    summed = summed.reshape(n_dev, n_dyl, 2 * k_blk * cols_here).astype(jnp.bfloat16)

    summed = lax.all_to_all(summed, ("scol", "srow"), split_axis=0, concat_axis=0, tiled=True)

    a_idx = lax.axis_index("scol")
    b_idx = lax.axis_index("srow")
    col_ids = jnp.arange(col_count, dtype=jnp.int32)
    my_j = b_idx * j_blk + jnp.arange(j_blk, dtype=jnp.int32)
    src_cos, src_sin = waves(jnp.arange(n_dev, dtype=jnp.int32) * cols_here, my_j, col_count)
    by_source = jnp.dot(
        summed.reshape(n_dev, -1).T.astype(jnp.float32),
        jnp.concatenate([src_cos, src_sin], axis=1),
        precision=HIGHEST,
        preferred_element_type=jnp.float32,
    ).reshape(n_dyl, 2, k_blk, cols_here, 2, j_blk)
    part_re = by_source[:, 0, :, :, 0] + by_source[:, 1, :, :, 1]
    part_im = by_source[:, 1, :, :, 0] - by_source[:, 0, :, :, 1]
    tw_cos, tw_sin = waves(jnp.arange(cols_here, dtype=jnp.int32), my_j, col_count)
    tw_cos = tw_cos[None, None, :, :]
    tw_sin = tw_sin[None, None, :, :]
    per_shift_re = jnp.sum(part_re * tw_cos + part_im * tw_sin, axis=2)
    per_shift_im = jnp.sum(part_im * tw_cos - part_re * tw_sin, axis=2)
    my_start = jnp.array(dy_first, dtype=jnp.int32)[b_idx]
    pick = (shift_index(my_j, col_count) - 2 * RAD - my_start)[None, :] == jnp.arange(n_dyl, dtype=jnp.int32)[:, None]
    pick = pick[:, None, :]
    psi = jnp.stack(
        [
            jnp.sum(jnp.where(pick, per_shift_re, 0.0), axis=0),
            jnp.sum(jnp.where(pick, per_shift_im, 0.0), axis=0),
        ],
        axis=1,
    )

    my_k = a_idx * k_blk + jnp.arange(k_blk, dtype=jnp.int32)
    inv_cos, inv_sin = waves(row_ids, my_k, row_count)
    inverse_rows = jnp.concatenate(
        [
            jnp.concatenate([inv_cos, -inv_sin], axis=1),
            jnp.concatenate([inv_sin, inv_cos], axis=1),
        ],
        axis=0,
    )
    psi = psi.transpose(1, 0, 2).reshape(2 * k_blk, j_blk)
    half = jnp.dot(inverse_rows, psi, precision=HIGHEST, preferred_element_type=jnp.float32)
    half = half.reshape(2, n_scol, row_count // n_scol, j_blk).transpose(1, 0, 2, 3)
    half = lax.all_to_all(half.astype(jnp.bfloat16), "scol", split_axis=0, concat_axis=0, tiled=True)
    half = jnp.sum(half.astype(jnp.float32), axis=0)
    out_rows = half.shape[1]

    out_cols = col_count // n_srow
    inv_cos, inv_sin = waves(my_j, col_ids, col_count)
    inverse_cols = jnp.concatenate(
        [
            jnp.concatenate([inv_cos, inv_sin], axis=1),
            jnp.concatenate([-inv_sin, inv_cos], axis=1),
        ],
        axis=0,
    )
    half = half.transpose(1, 0, 2).reshape(out_rows, 2 * j_blk)
    image = jnp.dot(half, inverse_cols, precision=HIGHEST, preferred_element_type=jnp.float32)
    image = image.reshape(out_rows, 2, n_srow, out_cols).transpose(2, 0, 1, 3)
    image = lax.all_to_all(image.astype(jnp.bfloat16), "srow", split_axis=0, concat_axis=0, tiled=True)
    image = jnp.sum(image.astype(jnp.float32), axis=0) * (1.0 / (row_count * col_count))
    return image


def solution(mesh):
    placed = (P("srow", "scol", None), P(), P(), P())
    return jax.shard_map(
        on_device, mesh=mesh, in_specs=placed, out_specs=P("scol", None, "srow"), check_vma=False
    )
```

```python
import math

import jax
import jax.numpy as jnp
from jax import lax
from jax.sharding import PartitionSpec as P

DET = 32
RAD = 13
HIGHEST = lax.Precision.HIGHEST


def waves(left_ids, right_ids, length):
    product = left_ids[:, None] * right_ids[None, :] % length
    phases = product.astype(jnp.float32) * (2.0 * math.pi / length)
    return (jnp.cos(phases), jnp.sin(phases))


def square_waves(count):
    minor = min(128, count)
    ids = jnp.arange(count, dtype=jnp.int32)
    major_cos, major_sin = waves(ids, jnp.arange(count // minor, dtype=jnp.int32) * minor, count)
    minor_cos, minor_sin = waves(ids, jnp.arange(minor, dtype=jnp.int32), count)
    major_cos = jnp.repeat(major_cos, minor, axis=1)
    major_sin = jnp.repeat(major_sin, minor, axis=1)
    minor_cos = jnp.tile(minor_cos, (1, count // minor))
    minor_sin = jnp.tile(minor_sin, (1, count // minor))
    return (
        major_cos * minor_cos - major_sin * minor_sin,
        major_sin * minor_cos + major_cos * minor_sin,
    )


def shift_index(freq, count):
    signed = jnp.where(freq >= count // 2, freq - count, freq)
    return signed * (4 * RAD) // count + 2 * RAD


def split_dot(left, right):
    hi = lax.reduce_precision(left, exponent_bits=8, mantissa_bits=7)
    lo = left - hi
    return jnp.dot(hi.astype(jnp.bfloat16), right, preferred_element_type=jnp.float32) + jnp.dot(
        lo.astype(jnp.bfloat16), right, preferred_element_type=jnp.float32
    )


def on_device(frames, pixel_gain, eigen_flats, pixels):
    n_srow = lax.axis_size("srow")
    n_scol = lax.axis_size("scol")
    n_dev = n_srow * n_scol
    local_rows, local_cols, n_pix = frames.shape
    row_count = local_rows * n_srow
    col_count = local_cols * n_scol
    n_shift = 4 * RAD
    flat_index = lax.axis_index("scol") * n_srow + lax.axis_index("srow")

    readings = frames.astype(jnp.float32)
    exposure = jnp.mean(readings, axis=2, keepdims=True)
    scaled = readings * pixel_gain / exposure
    fit_weights = jnp.einsum("rcp,ep->rce", scaled, eigen_flats, precision=lax.Precision.HIGH)
    fitted = jnp.einsum("rce,ep->rcp", fit_weights, eigen_flats, precision=lax.Precision.HIGH)
    flattened = (scaled - fitted).astype(jnp.bfloat16)

    cols_here = local_cols // n_srow
    me = lax.axis_index("srow")
    blocks = [lax.dynamic_slice_in_dim(flattened, me * cols_here, cols_here, axis=1)]
    for shift in range(1, n_srow):
        dest = (me + shift) % n_srow
        chunk = lax.dynamic_slice_in_dim(flattened, dest * cols_here, cols_here, axis=1)
        perm = [(i, (i + shift) % n_srow) for i in range(n_srow)]
        blocks.append(lax.ppermute(chunk, "srow", perm))
    gathered = jnp.concatenate(blocks, axis=0)

    k_blk = row_count // n_scol
    j_blk = col_count // n_srow
    row_ids = jnp.arange(row_count, dtype=jnp.int32)
    row_cos, row_sin = square_waves(row_count)
    src_rows = ((me - jnp.arange(n_srow, dtype=jnp.int32)) % n_srow)[:, None] * local_rows
    src_rows = (src_rows + jnp.arange(local_rows, dtype=jnp.int32)[None, :]).reshape(row_count)
    shifted_cos, shifted_sin = waves(row_ids, src_rows, row_count)
    forward_rows = jnp.stack([shifted_cos, -shifted_sin], axis=0).reshape(2, n_scol, k_blk, row_count)
    forward_rows = forward_rows.transpose(1, 0, 2, 3).reshape(2 * row_count, row_count)
    spec = jnp.dot(
        forward_rows.astype(jnp.bfloat16),
        gathered.reshape(row_count, cols_here * n_pix),
        preferred_element_type=jnp.float32,
    ).astype(jnp.bfloat16)
    spec = spec.reshape(n_scol, 2 * k_blk * cols_here, n_pix)

    def shift_of(freq, count):
        signed = freq - count if freq >= count // 2 else freq
        return (signed * (4 * RAD)) // count

    dx_first, dy_first = [], []
    for a in range(n_scol):
        shifts = [shift_of(k, row_count) for k in range(a * k_blk, (a + 1) * k_blk)]
        dx_first.append(min(shifts))
    n_dx = max(
        max(shift_of(k, row_count) for k in range(a * k_blk, (a + 1) * k_blk)) - dx_first[a] + 1
        for a in range(n_scol)
    )
    for b in range(n_srow):
        dy_first.append(min(shift_of(j, col_count) for j in range(b * j_blk, (b + 1) * j_blk)))
    n_dyl = max(
        max(shift_of(j, col_count) for j in range(b * j_blk, (b + 1) * j_blk)) - dy_first[b] + 1
        for b in range(n_srow)
    )
    n_dyl = -(-n_dyl // 8) * 8
    move_x = (jnp.array(dx_first, dtype=jnp.int32)[:, None] + jnp.arange(n_dx, dtype=jnp.int32)[None, :])
    move_y = (jnp.array(dy_first, dtype=jnp.int32)[:, None] + jnp.arange(n_dyl, dtype=jnp.int32)[None, :])
    move_x = move_x[:, None, None, :, None]
    move_y = move_y[None, :, :, None, None]
    det_x = (pixels % DET - DET // 2)[None, None, None, None, :]
    det_y = (pixels // DET - DET // 2)[None, None, None, None, :]
    upper = (det_x - move_x) * (det_x - move_x) + (det_y - move_y) * (det_y - move_y) <= RAD * RAD
    lower = (det_x + move_x) * (det_x + move_x) + (det_y + move_y) * (det_y + move_y) <= RAD * RAD
    weight = (upper.astype(jnp.float32) - lower.astype(jnp.float32)).astype(jnp.bfloat16)
    own_dx = (shift_index(row_ids, row_count) - 2 * RAD).reshape(n_scol, k_blk)
    own_dx = own_dx - jnp.array(dx_first, dtype=jnp.int32)[:, None]
    dx_of_n = jnp.broadcast_to(own_dx[:, None, :, None], (n_scol, 2, k_blk, cols_here))
    dx_of_n = dx_of_n.reshape(n_scol, 1, 2 * k_blk * cols_here)
    summed = None
    for d in range(n_dx):
        part = jnp.einsum(
            "axp,anp->axn",
            weight[:, :, :, d].reshape(n_scol, n_srow * n_dyl, n_pix),
            spec,
            preferred_element_type=jnp.float32,
        )
        part = jnp.where(dx_of_n == d, part, 0.0)
        summed = part if summed is None else summed + part
    summed = summed.reshape(n_dev, n_dyl, 2 * k_blk * cols_here).astype(jnp.bfloat16)

    summed = lax.all_to_all(summed, ("scol", "srow"), split_axis=0, concat_axis=0, tiled=True)

    a_idx = lax.axis_index("scol")
    b_idx = lax.axis_index("srow")
    col_ids = jnp.arange(col_count, dtype=jnp.int32)
    my_j = b_idx * j_blk + jnp.arange(j_blk, dtype=jnp.int32)
    src_cos, src_sin = waves(jnp.arange(n_dev, dtype=jnp.int32) * cols_here, my_j, col_count)
    by_source = jnp.dot(
        summed.reshape(n_dev, -1).T.astype(jnp.float32),
        jnp.concatenate([src_cos, src_sin], axis=1),
        precision=HIGHEST,
        preferred_element_type=jnp.float32,
    ).reshape(n_dyl, 2, k_blk, cols_here, 2, j_blk)
    part_re = by_source[:, 0, :, :, 0] + by_source[:, 1, :, :, 1]
    part_im = by_source[:, 1, :, :, 0] - by_source[:, 0, :, :, 1]
    tw_cos, tw_sin = waves(jnp.arange(cols_here, dtype=jnp.int32), my_j, col_count)
    tw_cos = tw_cos[None, None, :, :]
    tw_sin = tw_sin[None, None, :, :]
    per_shift_re = jnp.sum(part_re * tw_cos + part_im * tw_sin, axis=2)
    per_shift_im = jnp.sum(part_im * tw_cos - part_re * tw_sin, axis=2)
    my_start = jnp.array(dy_first, dtype=jnp.int32)[b_idx]
    pick = (shift_index(my_j, col_count) - 2 * RAD - my_start)[None, :] == jnp.arange(n_dyl, dtype=jnp.int32)[:, None]
    pick = pick[:, None, :]
    psi = jnp.stack(
        [
            jnp.sum(jnp.where(pick, per_shift_re, 0.0), axis=0),
            jnp.sum(jnp.where(pick, per_shift_im, 0.0), axis=0),
        ],
        axis=1,
    )

    my_k = a_idx * k_blk + jnp.arange(k_blk, dtype=jnp.int32)
    inv_cos, inv_sin = waves(row_ids, my_k, row_count)
    inverse_rows = jnp.concatenate(
        [
            jnp.concatenate([inv_cos, -inv_sin], axis=1),
            jnp.concatenate([inv_sin, inv_cos], axis=1),
        ],
        axis=0,
    )
    psi = psi.transpose(1, 0, 2).reshape(2 * k_blk, j_blk)
    half = jnp.dot(inverse_rows, psi, precision=HIGHEST, preferred_element_type=jnp.float32)
    half = half.reshape(2, n_scol, row_count // n_scol, j_blk).transpose(1, 0, 2, 3)
    half = lax.all_to_all(half.astype(jnp.bfloat16), "scol", split_axis=0, concat_axis=0, tiled=True)
    half = jnp.sum(half.astype(jnp.float32), axis=0)
    out_rows = half.shape[1]

    out_cols = col_count // n_srow
    inv_cos, inv_sin = waves(my_j, col_ids, col_count)
    inverse_cols = jnp.concatenate(
        [
            jnp.concatenate([inv_cos, inv_sin], axis=1),
            jnp.concatenate([-inv_sin, inv_cos], axis=1),
        ],
        axis=0,
    )
    half = half.transpose(1, 0, 2).reshape(out_rows, 2 * j_blk)
    image = jnp.dot(half, inverse_cols, precision=HIGHEST, preferred_element_type=jnp.float32)
    image = image.reshape(out_rows, 2, n_srow, out_cols).transpose(2, 0, 1, 3)
    image = lax.all_to_all(image.astype(jnp.bfloat16), "srow", split_axis=0, concat_axis=0, tiled=True)
    image = jnp.sum(image.astype(jnp.float32), axis=0) * (1.0 / (row_count * col_count))
    return image


def solution(mesh):
    placed = (P("srow", "scol", None), P(), P(), P())
    return jax.shard_map(
        on_device, mesh=mesh, in_specs=placed, out_specs=P("scol", None, "srow"), check_vma=False
    )
```

```python
import math

import jax
import jax.numpy as jnp
from jax import lax
from jax.sharding import PartitionSpec as P

DET = 32
RAD = 13
HIGHEST = lax.Precision.HIGHEST


def waves(left_ids, right_ids, length):
    product = left_ids[:, None] * right_ids[None, :] % length
    phases = product.astype(jnp.float32) * (2.0 * math.pi / length)
    return (jnp.cos(phases), jnp.sin(phases))


def square_waves(count):
    minor = min(128, count)
    ids = jnp.arange(count, dtype=jnp.int32)
    major_cos, major_sin = waves(ids, jnp.arange(count // minor, dtype=jnp.int32) * minor, count)
    minor_cos, minor_sin = waves(ids, jnp.arange(minor, dtype=jnp.int32), count)
    major_cos = jnp.repeat(major_cos, minor, axis=1)
    major_sin = jnp.repeat(major_sin, minor, axis=1)
    minor_cos = jnp.tile(minor_cos, (1, count // minor))
    minor_sin = jnp.tile(minor_sin, (1, count // minor))
    return (
        major_cos * minor_cos - major_sin * minor_sin,
        major_sin * minor_cos + major_cos * minor_sin,
    )


def shift_index(freq, count):
    signed = jnp.where(freq >= count // 2, freq - count, freq)
    return signed * (4 * RAD) // count + 2 * RAD


def split_dot(left, right):
    hi = lax.reduce_precision(left, exponent_bits=8, mantissa_bits=7)
    lo = left - hi
    return jnp.dot(hi.astype(jnp.bfloat16), right, preferred_element_type=jnp.float32) + jnp.dot(
        lo.astype(jnp.bfloat16), right, preferred_element_type=jnp.float32
    )


def on_device(frames, pixel_gain, eigen_flats, pixels):
    n_srow = lax.axis_size("srow")
    n_scol = lax.axis_size("scol")
    n_dev = n_srow * n_scol
    local_rows, local_cols, n_pix = frames.shape
    row_count = local_rows * n_srow
    col_count = local_cols * n_scol
    n_shift = 4 * RAD
    flat_index = lax.axis_index("scol") * n_srow + lax.axis_index("srow")

    readings = frames.astype(jnp.float32)
    exposure = jnp.mean(readings, axis=2, keepdims=True)
    scaled = readings * pixel_gain / exposure
    fit_weights = jnp.einsum("rcp,ep->rce", scaled, eigen_flats, precision=lax.Precision.HIGH)
    fitted = jnp.einsum("rce,ep->rcp", fit_weights, eigen_flats, precision=lax.Precision.HIGH)
    flattened = (scaled - fitted).astype(jnp.bfloat16)

    gathered = lax.all_to_all(flattened, "srow", split_axis=1, concat_axis=0, tiled=True)
    cols_here = gathered.shape[1]

    k_blk = row_count // n_scol
    j_blk = col_count // n_srow
    row_ids = jnp.arange(row_count, dtype=jnp.int32)
    row_cos, row_sin = square_waves(row_count)
    forward_rows = jnp.stack([row_cos, -row_sin], axis=0).reshape(2, n_scol, k_blk, row_count)
    forward_rows = forward_rows.transpose(1, 0, 2, 3).reshape(2 * row_count, row_count)
    spec = jnp.dot(
        forward_rows.astype(jnp.bfloat16),
        gathered.reshape(row_count, cols_here * n_pix),
        preferred_element_type=jnp.float32,
    ).astype(jnp.bfloat16)
    spec = spec.reshape(n_scol, 2 * k_blk * cols_here, n_pix)

    def shift_of(freq, count):
        signed = freq - count if freq >= count // 2 else freq
        return (signed * (4 * RAD)) // count

    dx_first, dy_first = [], []
    for a in range(n_scol):
        shifts = [shift_of(k, row_count) for k in range(a * k_blk, (a + 1) * k_blk)]
        dx_first.append(min(shifts))
    n_dx = max(
        max(shift_of(k, row_count) for k in range(a * k_blk, (a + 1) * k_blk)) - dx_first[a] + 1
        for a in range(n_scol)
    )
    for b in range(n_srow):
        dy_first.append(min(shift_of(j, col_count) for j in range(b * j_blk, (b + 1) * j_blk)))
    n_dyl = max(
        max(shift_of(j, col_count) for j in range(b * j_blk, (b + 1) * j_blk)) - dy_first[b] + 1
        for b in range(n_srow)
    )
    n_dyl = -(-n_dyl // 8) * 8
    move_x = (jnp.array(dx_first, dtype=jnp.int32)[:, None] + jnp.arange(n_dx, dtype=jnp.int32)[None, :])
    move_y = (jnp.array(dy_first, dtype=jnp.int32)[:, None] + jnp.arange(n_dyl, dtype=jnp.int32)[None, :])
    move_x = move_x[:, None, None, :, None]
    move_y = move_y[None, :, :, None, None]
    det_x = (pixels % DET - DET // 2)[None, None, None, None, :]
    det_y = (pixels // DET - DET // 2)[None, None, None, None, :]
    upper = (det_x - move_x) * (det_x - move_x) + (det_y - move_y) * (det_y - move_y) <= RAD * RAD
    lower = (det_x + move_x) * (det_x + move_x) + (det_y + move_y) * (det_y + move_y) <= RAD * RAD
    weight = (upper.astype(jnp.float32) - lower.astype(jnp.float32)).astype(jnp.bfloat16)
    own_dx = (shift_index(row_ids, row_count) - 2 * RAD).reshape(n_scol, k_blk)
    own_dx = own_dx - jnp.array(dx_first, dtype=jnp.int32)[:, None]
    dx_of_n = jnp.broadcast_to(own_dx[:, None, :, None], (n_scol, 2, k_blk, cols_here))
    dx_of_n = dx_of_n.reshape(n_scol, 1, 2 * k_blk * cols_here)
    summed = None
    for d in range(n_dx):
        part = jnp.einsum(
            "axp,anp->axn",
            weight[:, :, :, d].reshape(n_scol, n_srow * n_dyl, n_pix),
            spec,
            preferred_element_type=jnp.float32,
        )
        part = jnp.where(dx_of_n == d, part, 0.0)
        summed = part if summed is None else summed + part
    summed = summed.reshape(n_dev, n_dyl, 2 * k_blk * cols_here).astype(jnp.bfloat16)

    summed = lax.all_to_all(summed, ("scol", "srow"), split_axis=0, concat_axis=0, tiled=True)

    a_idx = lax.axis_index("scol")
    b_idx = lax.axis_index("srow")
    col_ids = jnp.arange(col_count, dtype=jnp.int32)
    my_j = b_idx * j_blk + jnp.arange(j_blk, dtype=jnp.int32)
    src_cos, src_sin = waves(jnp.arange(n_dev, dtype=jnp.int32) * cols_here, my_j, col_count)
    by_source = jnp.dot(
        summed.reshape(n_dev, -1).T.astype(jnp.float32),
        jnp.concatenate([src_cos, src_sin], axis=1),
        precision=lax.Precision.HIGH,
        preferred_element_type=jnp.float32,
    ).reshape(n_dyl, 2, k_blk, cols_here, 2, j_blk)
    part_re = by_source[:, 0, :, :, 0] + by_source[:, 1, :, :, 1]
    part_im = by_source[:, 1, :, :, 0] - by_source[:, 0, :, :, 1]
    tw_cos, tw_sin = waves(jnp.arange(cols_here, dtype=jnp.int32), my_j, col_count)
    tw_cos = tw_cos[None, None, :, :]
    tw_sin = tw_sin[None, None, :, :]
    per_shift_re = jnp.sum(part_re * tw_cos + part_im * tw_sin, axis=2)
    per_shift_im = jnp.sum(part_im * tw_cos - part_re * tw_sin, axis=2)
    my_start = jnp.array(dy_first, dtype=jnp.int32)[b_idx]
    pick = (shift_index(my_j, col_count) - 2 * RAD - my_start)[None, :] == jnp.arange(n_dyl, dtype=jnp.int32)[:, None]
    pick = pick[:, None, :]
    psi = jnp.stack(
        [
            jnp.sum(jnp.where(pick, per_shift_re, 0.0), axis=0),
            jnp.sum(jnp.where(pick, per_shift_im, 0.0), axis=0),
        ],
        axis=1,
    )

    my_k = a_idx * k_blk + jnp.arange(k_blk, dtype=jnp.int32)
    inv_cos, inv_sin = waves(row_ids, my_k, row_count)
    inverse_rows = jnp.concatenate(
        [
            jnp.concatenate([inv_cos, -inv_sin], axis=1),
            jnp.concatenate([inv_sin, inv_cos], axis=1),
        ],
        axis=0,
    )
    psi = psi.transpose(1, 0, 2).reshape(2 * k_blk, j_blk)
    half = jnp.dot(inverse_rows, psi, precision=lax.Precision.HIGH, preferred_element_type=jnp.float32)
    half = half.reshape(2, n_scol, row_count // n_scol, j_blk).transpose(1, 0, 2, 3)
    half = lax.all_to_all(half.astype(jnp.bfloat16), "scol", split_axis=0, concat_axis=0, tiled=True)
    half = jnp.sum(half.astype(jnp.float32), axis=0)
    out_rows = half.shape[1]

    out_cols = col_count // n_srow
    inv_cos, inv_sin = waves(my_j, col_ids, col_count)
    inverse_cols = jnp.concatenate(
        [
            jnp.concatenate([inv_cos, inv_sin], axis=1),
            jnp.concatenate([-inv_sin, inv_cos], axis=1),
        ],
        axis=0,
    )
    half = half.transpose(1, 0, 2).reshape(out_rows, 2 * j_blk)
    image = jnp.dot(half, inverse_cols, precision=lax.Precision.HIGH, preferred_element_type=jnp.float32)
    image = image.reshape(out_rows, 2, n_srow, out_cols).transpose(2, 0, 1, 3)
    image = lax.all_to_all(image.astype(jnp.bfloat16), "srow", split_axis=0, concat_axis=0, tiled=True)
    image = jnp.sum(image.astype(jnp.float32), axis=0) * (1.0 / (row_count * col_count))
    return image


def solution(mesh):
    placed = (P("srow", "scol", None), P(), P(), P())
    return jax.shard_map(
        on_device, mesh=mesh, in_specs=placed, out_specs=P("scol", None, "srow"), check_vma=False
    )
```

```python
import math

import jax
import jax.numpy as jnp
from jax import lax
from jax.sharding import PartitionSpec as P

DET = 32
RAD = 13
HIGHEST = lax.Precision.HIGHEST


def waves(left_ids, right_ids, length):
    product = left_ids[:, None] * right_ids[None, :] % length
    phases = product.astype(jnp.float32) * (2.0 * math.pi / length)
    return (jnp.cos(phases), jnp.sin(phases))


def square_waves(count):
    minor = min(128, count)
    ids = jnp.arange(count, dtype=jnp.int32)
    major_cos, major_sin = waves(ids, jnp.arange(count // minor, dtype=jnp.int32) * minor, count)
    minor_cos, minor_sin = waves(ids, jnp.arange(minor, dtype=jnp.int32), count)
    major_cos = jnp.repeat(major_cos, minor, axis=1)
    major_sin = jnp.repeat(major_sin, minor, axis=1)
    minor_cos = jnp.tile(minor_cos, (1, count // minor))
    minor_sin = jnp.tile(minor_sin, (1, count // minor))
    return (
        major_cos * minor_cos - major_sin * minor_sin,
        major_sin * minor_cos + major_cos * minor_sin,
    )


def shift_index(freq, count):
    signed = jnp.where(freq >= count // 2, freq - count, freq)
    return signed * (4 * RAD) // count + 2 * RAD


def split_dot(left, right):
    hi = lax.reduce_precision(left, exponent_bits=8, mantissa_bits=7)
    lo = left - hi
    return jnp.dot(hi.astype(jnp.bfloat16), right, preferred_element_type=jnp.float32) + jnp.dot(
        lo.astype(jnp.bfloat16), right, preferred_element_type=jnp.float32
    )


def on_device(frames, pixel_gain, eigen_flats, pixels):
    n_srow = lax.axis_size("srow")
    n_scol = lax.axis_size("scol")
    n_dev = n_srow * n_scol
    local_rows, local_cols, n_pix = frames.shape
    row_count = local_rows * n_srow
    col_count = local_cols * n_scol
    n_shift = 4 * RAD
    flat_index = lax.axis_index("scol") * n_srow + lax.axis_index("srow")

    readings = frames.astype(jnp.float32)
    exposure = jnp.mean(readings, axis=2, keepdims=True)
    scaled = readings * pixel_gain / exposure
    fit_weights = jnp.einsum("rcp,ep->rce", scaled, eigen_flats, precision=lax.Precision.HIGH)
    fitted = jnp.einsum("rce,ep->rcp", fit_weights, eigen_flats, precision=lax.Precision.HIGH)
    flattened = (scaled - fitted).astype(jnp.bfloat16)

    gathered = lax.all_to_all(flattened, "srow", split_axis=1, concat_axis=0, tiled=True)
    cols_here = gathered.shape[1]

    k_blk = row_count // n_scol
    j_blk = col_count // n_srow
    row_ids = jnp.arange(row_count, dtype=jnp.int32)
    row_cos, row_sin = square_waves(row_count)
    forward_rows = jnp.stack([row_cos, -row_sin], axis=0).reshape(2, n_scol, k_blk, row_count)
    forward_rows = forward_rows.transpose(1, 0, 2, 3).reshape(2 * row_count, row_count)
    spec = jnp.dot(
        forward_rows.astype(jnp.bfloat16),
        gathered.reshape(row_count, cols_here * n_pix),
        preferred_element_type=jnp.float32,
    ).astype(jnp.bfloat16)
    spec = spec.reshape(n_scol, 2 * k_blk * cols_here, n_pix)

    def shift_of(freq, count):
        signed = freq - count if freq >= count // 2 else freq
        return (signed * (4 * RAD)) // count

    dx_first, dy_first = [], []
    for a in range(n_scol):
        shifts = [shift_of(k, row_count) for k in range(a * k_blk, (a + 1) * k_blk)]
        dx_first.append(min(shifts))
    n_dx = max(
        max(shift_of(k, row_count) for k in range(a * k_blk, (a + 1) * k_blk)) - dx_first[a] + 1
        for a in range(n_scol)
    )
    for b in range(n_srow):
        dy_first.append(min(shift_of(j, col_count) for j in range(b * j_blk, (b + 1) * j_blk)))
    n_dyl = max(
        max(shift_of(j, col_count) for j in range(b * j_blk, (b + 1) * j_blk)) - dy_first[b] + 1
        for b in range(n_srow)
    )
    n_dyl = -(-n_dyl // 8) * 8
    move_x = (jnp.array(dx_first, dtype=jnp.int32)[:, None] + jnp.arange(n_dx, dtype=jnp.int32)[None, :])
    move_y = (jnp.array(dy_first, dtype=jnp.int32)[:, None] + jnp.arange(n_dyl, dtype=jnp.int32)[None, :])
    move_x = move_x[:, None, None, :, None]
    move_y = move_y[None, :, :, None, None]
    det_x = (pixels % DET - DET // 2)[None, None, None, None, :]
    det_y = (pixels // DET - DET // 2)[None, None, None, None, :]
    upper = (det_x - move_x) * (det_x - move_x) + (det_y - move_y) * (det_y - move_y) <= RAD * RAD
    lower = (det_x + move_x) * (det_x + move_x) + (det_y + move_y) * (det_y + move_y) <= RAD * RAD
    weight = (upper.astype(jnp.float32) - lower.astype(jnp.float32)).astype(jnp.bfloat16)
    own_dx = (shift_index(row_ids, row_count) - 2 * RAD).reshape(n_scol, k_blk)
    own_dx = own_dx - jnp.array(dx_first, dtype=jnp.int32)[:, None]
    dx_of_n = jnp.broadcast_to(own_dx[:, None, :, None], (n_scol, 2, k_blk, cols_here))
    dx_of_n = dx_of_n.reshape(n_scol, 1, 2 * k_blk * cols_here)
    weight = weight.transpose(0, 3, 1, 2, 4).reshape(n_scol, n_dx * n_srow * n_dyl, n_pix)
    every_dx = jnp.einsum("axp,anp->axn", weight, spec, preferred_element_type=jnp.float32)
    every_dx = every_dx.reshape(n_scol, n_dx, n_srow * n_dyl, 2 * k_blk * cols_here)
    dx_pick = dx_of_n[:, None, :, :] == jnp.arange(n_dx, dtype=jnp.int32)[None, :, None, None]
    summed = jnp.sum(jnp.where(dx_pick, every_dx, 0.0), axis=1)
    summed = summed.reshape(n_dev, n_dyl, 2 * k_blk * cols_here).astype(jnp.bfloat16)

    summed = lax.all_to_all(summed, ("scol", "srow"), split_axis=0, concat_axis=0, tiled=True)

    a_idx = lax.axis_index("scol")
    b_idx = lax.axis_index("srow")
    col_ids = jnp.arange(col_count, dtype=jnp.int32)
    my_j = b_idx * j_blk + jnp.arange(j_blk, dtype=jnp.int32)
    src_cos, src_sin = waves(jnp.arange(n_dev, dtype=jnp.int32) * cols_here, my_j, col_count)
    by_source = jnp.dot(
        summed.reshape(n_dev, -1).T.astype(jnp.float32),
        jnp.concatenate([src_cos, src_sin], axis=1),
        precision=lax.Precision.HIGH,
        preferred_element_type=jnp.float32,
    ).reshape(n_dyl, 2, k_blk, cols_here, 2, j_blk)
    part_re = by_source[:, 0, :, :, 0] + by_source[:, 1, :, :, 1]
    part_im = by_source[:, 1, :, :, 0] - by_source[:, 0, :, :, 1]
    tw_cos, tw_sin = waves(jnp.arange(cols_here, dtype=jnp.int32), my_j, col_count)
    tw_cos = tw_cos[None, None, :, :]
    tw_sin = tw_sin[None, None, :, :]
    per_shift_re = jnp.sum(part_re * tw_cos + part_im * tw_sin, axis=2)
    per_shift_im = jnp.sum(part_im * tw_cos - part_re * tw_sin, axis=2)
    my_start = jnp.array(dy_first, dtype=jnp.int32)[b_idx]
    pick = (shift_index(my_j, col_count) - 2 * RAD - my_start)[None, :] == jnp.arange(n_dyl, dtype=jnp.int32)[:, None]
    pick = pick[:, None, :]
    psi = jnp.stack(
        [
            jnp.sum(jnp.where(pick, per_shift_re, 0.0), axis=0),
            jnp.sum(jnp.where(pick, per_shift_im, 0.0), axis=0),
        ],
        axis=1,
    )

    my_k = a_idx * k_blk + jnp.arange(k_blk, dtype=jnp.int32)
    inv_cos, inv_sin = waves(row_ids, my_k, row_count)
    inverse_rows = jnp.concatenate(
        [
            jnp.concatenate([inv_cos, -inv_sin], axis=1),
            jnp.concatenate([inv_sin, inv_cos], axis=1),
        ],
        axis=0,
    )
    psi = psi.transpose(1, 0, 2).reshape(2 * k_blk, j_blk)
    half = jnp.dot(inverse_rows, psi, precision=lax.Precision.HIGH, preferred_element_type=jnp.float32)
    half = half.reshape(2, n_scol, row_count // n_scol, j_blk).transpose(1, 0, 2, 3)
    half = lax.all_to_all(half.astype(jnp.bfloat16), "scol", split_axis=0, concat_axis=0, tiled=True)
    half = jnp.sum(half.astype(jnp.float32), axis=0)
    out_rows = half.shape[1]

    out_cols = col_count // n_srow
    inv_cos, inv_sin = waves(my_j, col_ids, col_count)
    inverse_cols = jnp.concatenate(
        [
            jnp.concatenate([inv_cos, inv_sin], axis=1),
            jnp.concatenate([-inv_sin, inv_cos], axis=1),
        ],
        axis=0,
    )
    half = half.transpose(1, 0, 2).reshape(out_rows, 2 * j_blk)
    image = jnp.dot(half, inverse_cols, precision=lax.Precision.HIGH, preferred_element_type=jnp.float32)
    image = image.reshape(out_rows, 2, n_srow, out_cols).transpose(2, 0, 1, 3)
    image = lax.all_to_all(image.astype(jnp.bfloat16), "srow", split_axis=0, concat_axis=0, tiled=True)
    image = jnp.sum(image.astype(jnp.float32), axis=0) * (1.0 / (row_count * col_count))
    return image


def solution(mesh):
    placed = (P("srow", "scol", None), P(), P(), P())
    return jax.shard_map(
        on_device, mesh=mesh, in_specs=placed, out_specs=P("scol", None, "srow"), check_vma=False
    )
```

```python
import math

import jax
import jax.numpy as jnp
from jax import lax
from jax.sharding import PartitionSpec as P

DET = 32
RAD = 13
HIGHEST = lax.Precision.HIGHEST


def waves(left_ids, right_ids, length):
    product = left_ids[:, None] * right_ids[None, :] % length
    phases = product.astype(jnp.float32) * (2.0 * math.pi / length)
    return (jnp.cos(phases), jnp.sin(phases))


def square_waves(count):
    minor = min(128, count)
    ids = jnp.arange(count, dtype=jnp.int32)
    major_cos, major_sin = waves(ids, jnp.arange(count // minor, dtype=jnp.int32) * minor, count)
    minor_cos, minor_sin = waves(ids, jnp.arange(minor, dtype=jnp.int32), count)
    major_cos = jnp.repeat(major_cos, minor, axis=1)
    major_sin = jnp.repeat(major_sin, minor, axis=1)
    minor_cos = jnp.tile(minor_cos, (1, count // minor))
    minor_sin = jnp.tile(minor_sin, (1, count // minor))
    return (
        major_cos * minor_cos - major_sin * minor_sin,
        major_sin * minor_cos + major_cos * minor_sin,
    )


def shift_index(freq, count):
    signed = jnp.where(freq >= count // 2, freq - count, freq)
    return signed * (4 * RAD) // count + 2 * RAD


def split_dot(left, right):
    hi = lax.reduce_precision(left, exponent_bits=8, mantissa_bits=7)
    lo = left - hi
    return jnp.dot(hi.astype(jnp.bfloat16), right, preferred_element_type=jnp.float32) + jnp.dot(
        lo.astype(jnp.bfloat16), right, preferred_element_type=jnp.float32
    )


def on_device(frames, pixel_gain, eigen_flats, pixels):
    n_srow = lax.axis_size("srow")
    n_scol = lax.axis_size("scol")
    n_dev = n_srow * n_scol
    local_rows, local_cols, n_pix = frames.shape
    row_count = local_rows * n_srow
    col_count = local_cols * n_scol
    n_shift = 4 * RAD
    flat_index = lax.axis_index("scol") * n_srow + lax.axis_index("srow")

    readings = frames.astype(jnp.float32)
    exposure = jnp.mean(readings, axis=2, keepdims=True)
    scaled = readings * pixel_gain / exposure
    fit_weights = jnp.einsum("rcp,ep->rce", scaled, eigen_flats, precision=lax.Precision.HIGH)
    fitted = jnp.einsum("rce,ep->rcp", fit_weights, eigen_flats, precision=lax.Precision.HIGH)
    flattened = (scaled - fitted).astype(jnp.bfloat16)

    cols_here = local_cols // n_srow
    flattened = flattened.reshape(local_rows, n_srow, cols_here * n_pix).transpose(1, 0, 2)
    gathered = lax.all_to_all(flattened, "srow", split_axis=0, concat_axis=0, tiled=True)

    k_blk = row_count // n_scol
    j_blk = col_count // n_srow
    row_ids = jnp.arange(row_count, dtype=jnp.int32)
    row_cos, row_sin = square_waves(row_count)
    forward_rows = jnp.stack([row_cos, -row_sin], axis=0).reshape(2, n_scol, k_blk, row_count)
    forward_rows = forward_rows.transpose(1, 0, 2, 3).reshape(2 * row_count, row_count)
    spec = jnp.dot(
        forward_rows.astype(jnp.bfloat16),
        gathered.reshape(row_count, cols_here * n_pix),
        preferred_element_type=jnp.float32,
    ).astype(jnp.bfloat16)
    spec = spec.reshape(n_scol, 2 * k_blk * cols_here, n_pix)

    def shift_of(freq, count):
        signed = freq - count if freq >= count // 2 else freq
        return (signed * (4 * RAD)) // count

    dx_first, dy_first = [], []
    for a in range(n_scol):
        shifts = [shift_of(k, row_count) for k in range(a * k_blk, (a + 1) * k_blk)]
        dx_first.append(min(shifts))
    n_dx = max(
        max(shift_of(k, row_count) for k in range(a * k_blk, (a + 1) * k_blk)) - dx_first[a] + 1
        for a in range(n_scol)
    )
    for b in range(n_srow):
        dy_first.append(min(shift_of(j, col_count) for j in range(b * j_blk, (b + 1) * j_blk)))
    n_dyl = max(
        max(shift_of(j, col_count) for j in range(b * j_blk, (b + 1) * j_blk)) - dy_first[b] + 1
        for b in range(n_srow)
    )
    n_dyl = -(-n_dyl // 8) * 8
    move_x = (jnp.array(dx_first, dtype=jnp.int32)[:, None] + jnp.arange(n_dx, dtype=jnp.int32)[None, :])
    move_y = (jnp.array(dy_first, dtype=jnp.int32)[:, None] + jnp.arange(n_dyl, dtype=jnp.int32)[None, :])
    move_x = move_x[:, None, None, :, None]
    move_y = move_y[None, :, :, None, None]
    det_x = (pixels % DET - DET // 2)[None, None, None, None, :]
    det_y = (pixels // DET - DET // 2)[None, None, None, None, :]
    upper = (det_x - move_x) * (det_x - move_x) + (det_y - move_y) * (det_y - move_y) <= RAD * RAD
    lower = (det_x + move_x) * (det_x + move_x) + (det_y + move_y) * (det_y + move_y) <= RAD * RAD
    weight = (upper.astype(jnp.float32) - lower.astype(jnp.float32)).astype(jnp.bfloat16)
    own_dx = (shift_index(row_ids, row_count) - 2 * RAD).reshape(n_scol, k_blk)
    own_dx = own_dx - jnp.array(dx_first, dtype=jnp.int32)[:, None]
    dx_of_n = jnp.broadcast_to(own_dx[:, None, :, None], (n_scol, 2, k_blk, cols_here))
    dx_of_n = dx_of_n.reshape(n_scol, 1, 2 * k_blk * cols_here)
    weight = weight.transpose(0, 3, 1, 2, 4).reshape(n_scol, n_dx * n_srow * n_dyl, n_pix)
    every_dx = jnp.einsum("axp,anp->axn", weight, spec, preferred_element_type=jnp.float32)
    every_dx = every_dx.reshape(n_scol, n_dx, n_srow * n_dyl, 2 * k_blk * cols_here)
    dx_pick = dx_of_n[:, None, :, :] == jnp.arange(n_dx, dtype=jnp.int32)[None, :, None, None]
    summed = jnp.sum(jnp.where(dx_pick, every_dx, 0.0), axis=1)
    summed = summed.reshape(n_dev, n_dyl, 2 * k_blk * cols_here).astype(jnp.bfloat16)

    summed = lax.all_to_all(summed, ("scol", "srow"), split_axis=0, concat_axis=0, tiled=True)

    a_idx = lax.axis_index("scol")
    b_idx = lax.axis_index("srow")
    col_ids = jnp.arange(col_count, dtype=jnp.int32)
    my_j = b_idx * j_blk + jnp.arange(j_blk, dtype=jnp.int32)
    src_cos, src_sin = waves(jnp.arange(n_dev, dtype=jnp.int32) * cols_here, my_j, col_count)
    by_source = jnp.dot(
        summed.reshape(n_dev, -1).T.astype(jnp.float32),
        jnp.concatenate([src_cos, src_sin], axis=1),
        precision=lax.Precision.HIGH,
        preferred_element_type=jnp.float32,
    ).reshape(n_dyl, 2, k_blk, cols_here, 2, j_blk)
    part_re = by_source[:, 0, :, :, 0] + by_source[:, 1, :, :, 1]
    part_im = by_source[:, 1, :, :, 0] - by_source[:, 0, :, :, 1]
    tw_cos, tw_sin = waves(jnp.arange(cols_here, dtype=jnp.int32), my_j, col_count)
    tw_cos = tw_cos[None, None, :, :]
    tw_sin = tw_sin[None, None, :, :]
    per_shift_re = jnp.sum(part_re * tw_cos + part_im * tw_sin, axis=2)
    per_shift_im = jnp.sum(part_im * tw_cos - part_re * tw_sin, axis=2)
    my_start = jnp.array(dy_first, dtype=jnp.int32)[b_idx]
    pick = (shift_index(my_j, col_count) - 2 * RAD - my_start)[None, :] == jnp.arange(n_dyl, dtype=jnp.int32)[:, None]
    pick = pick[:, None, :]
    psi = jnp.stack(
        [
            jnp.sum(jnp.where(pick, per_shift_re, 0.0), axis=0),
            jnp.sum(jnp.where(pick, per_shift_im, 0.0), axis=0),
        ],
        axis=1,
    )

    my_k = a_idx * k_blk + jnp.arange(k_blk, dtype=jnp.int32)
    inv_cos, inv_sin = waves(row_ids, my_k, row_count)
    inverse_rows = jnp.concatenate(
        [
            jnp.concatenate([inv_cos, -inv_sin], axis=1),
            jnp.concatenate([inv_sin, inv_cos], axis=1),
        ],
        axis=0,
    )
    psi = psi.transpose(1, 0, 2).reshape(2 * k_blk, j_blk)
    half = jnp.dot(inverse_rows, psi, precision=lax.Precision.HIGH, preferred_element_type=jnp.float32)
    half = half.reshape(2, n_scol, row_count // n_scol, j_blk).transpose(1, 0, 2, 3)
    half = lax.all_to_all(half.astype(jnp.bfloat16), "scol", split_axis=0, concat_axis=0, tiled=True)
    half = jnp.sum(half.astype(jnp.float32), axis=0)
    out_rows = half.shape[1]

    out_cols = col_count // n_srow
    inv_cos, inv_sin = waves(my_j, col_ids, col_count)
    inverse_cols = jnp.concatenate(
        [
            jnp.concatenate([inv_cos, inv_sin], axis=1),
            jnp.concatenate([-inv_sin, inv_cos], axis=1),
        ],
        axis=0,
    )
    half = half.transpose(1, 0, 2).reshape(out_rows, 2 * j_blk)
    image = jnp.dot(half, inverse_cols, precision=lax.Precision.HIGH, preferred_element_type=jnp.float32)
    image = image.reshape(out_rows, 2, n_srow, out_cols).transpose(2, 0, 1, 3)
    image = lax.all_to_all(image.astype(jnp.bfloat16), "srow", split_axis=0, concat_axis=0, tiled=True)
    image = jnp.sum(image.astype(jnp.float32), axis=0) * (1.0 / (row_count * col_count))
    return image


def solution(mesh):
    placed = (P("srow", "scol", None), P(), P(), P())
    return jax.shard_map(
        on_device, mesh=mesh, in_specs=placed, out_specs=P("scol", None, "srow"), check_vma=False
    )
```

```python
import math

import jax
import jax.numpy as jnp
from jax import lax
from jax.sharding import PartitionSpec as P

DET = 32
RAD = 13
HIGHEST = lax.Precision.HIGHEST


def waves(left_ids, right_ids, length):
    product = left_ids[:, None] * right_ids[None, :] % length
    phases = product.astype(jnp.float32) * (2.0 * math.pi / length)
    return (jnp.cos(phases), jnp.sin(phases))


def square_waves(count):
    minor = min(128, count)
    ids = jnp.arange(count, dtype=jnp.int32)
    major_cos, major_sin = waves(ids, jnp.arange(count // minor, dtype=jnp.int32) * minor, count)
    minor_cos, minor_sin = waves(ids, jnp.arange(minor, dtype=jnp.int32), count)
    major_cos = jnp.repeat(major_cos, minor, axis=1)
    major_sin = jnp.repeat(major_sin, minor, axis=1)
    minor_cos = jnp.tile(minor_cos, (1, count // minor))
    minor_sin = jnp.tile(minor_sin, (1, count // minor))
    return (
        major_cos * minor_cos - major_sin * minor_sin,
        major_sin * minor_cos + major_cos * minor_sin,
    )


def shift_index(freq, count):
    signed = jnp.where(freq >= count // 2, freq - count, freq)
    return signed * (4 * RAD) // count + 2 * RAD


def split_dot(left, right):
    hi = lax.reduce_precision(left, exponent_bits=8, mantissa_bits=7)
    lo = left - hi
    return jnp.dot(hi.astype(jnp.bfloat16), right, preferred_element_type=jnp.float32) + jnp.dot(
        lo.astype(jnp.bfloat16), right, preferred_element_type=jnp.float32
    )


def on_device(frames, pixel_gain, eigen_flats, pixels):
    n_srow = lax.axis_size("srow")
    n_scol = lax.axis_size("scol")
    n_dev = n_srow * n_scol
    local_rows, local_cols, n_pix = frames.shape
    row_count = local_rows * n_srow
    col_count = local_cols * n_scol
    n_shift = 4 * RAD
    flat_index = lax.axis_index("scol") * n_srow + lax.axis_index("srow")

    readings = frames.astype(jnp.float32)
    exposure = jnp.mean(readings, axis=2, keepdims=True)
    scaled = readings * pixel_gain / exposure
    fit_weights = jnp.einsum("rcp,ep->rce", scaled, eigen_flats, precision=lax.Precision.HIGH)
    fitted = jnp.einsum("rce,ep->rcp", fit_weights, eigen_flats, precision=lax.Precision.HIGH)
    flattened = (scaled - fitted).astype(jnp.bfloat16)

    gathered = lax.all_to_all(flattened, "srow", split_axis=1, concat_axis=0, tiled=True)
    cols_here = gathered.shape[1]

    k_blk = row_count // n_scol
    j_blk = col_count // n_srow
    row_ids = jnp.arange(row_count, dtype=jnp.int32)
    row_cos, row_sin = square_waves(row_count)
    forward_rows = jnp.stack([row_cos, -row_sin], axis=0).reshape(2, n_scol, k_blk, row_count)
    forward_rows = forward_rows.transpose(1, 0, 2, 3).reshape(2 * row_count, row_count)
    spec = jnp.dot(
        forward_rows.astype(jnp.bfloat16),
        gathered.reshape(row_count, cols_here * n_pix),
        preferred_element_type=jnp.float32,
    ).astype(jnp.bfloat16)
    spec = spec.reshape(n_scol, 2 * k_blk * cols_here, n_pix)

    def shift_of(freq, count):
        signed = freq - count if freq >= count // 2 else freq
        return (signed * (4 * RAD)) // count

    dx_first, dy_first = [], []
    for a in range(n_scol):
        shifts = [shift_of(k, row_count) for k in range(a * k_blk, (a + 1) * k_blk)]
        dx_first.append(min(shifts))
    n_dx = max(
        max(shift_of(k, row_count) for k in range(a * k_blk, (a + 1) * k_blk)) - dx_first[a] + 1
        for a in range(n_scol)
    )
    for b in range(n_srow):
        dy_first.append(min(shift_of(j, col_count) for j in range(b * j_blk, (b + 1) * j_blk)))
    n_dyl = max(
        max(shift_of(j, col_count) for j in range(b * j_blk, (b + 1) * j_blk)) - dy_first[b] + 1
        for b in range(n_srow)
    )
    n_dyl = -(-n_dyl // 8) * 8
    move_x = (jnp.array(dx_first, dtype=jnp.int32)[:, None] + jnp.arange(n_dx, dtype=jnp.int32)[None, :])
    move_y = (jnp.array(dy_first, dtype=jnp.int32)[:, None] + jnp.arange(n_dyl, dtype=jnp.int32)[None, :])
    move_x = move_x[:, None, None, :, None]
    move_y = move_y[None, :, :, None, None]
    det_x = (pixels % DET - DET // 2)[None, None, None, None, :]
    det_y = (pixels // DET - DET // 2)[None, None, None, None, :]
    upper = (det_x - move_x) * (det_x - move_x) + (det_y - move_y) * (det_y - move_y) <= RAD * RAD
    lower = (det_x + move_x) * (det_x + move_x) + (det_y + move_y) * (det_y + move_y) <= RAD * RAD
    weight = (upper.astype(jnp.float32) - lower.astype(jnp.float32)).astype(jnp.bfloat16)
    own_dx = (shift_index(row_ids, row_count) - 2 * RAD).reshape(n_scol, k_blk)
    own_dx = own_dx - jnp.array(dx_first, dtype=jnp.int32)[:, None]
    dx_of_n = jnp.broadcast_to(own_dx[:, None, :, None], (n_scol, 2, k_blk, cols_here))
    dx_of_n = dx_of_n.reshape(n_scol, 1, 2 * k_blk * cols_here)
    weight = weight.transpose(0, 3, 1, 2, 4).reshape(n_scol, n_dx * n_srow * n_dyl, n_pix)
    every_dx = jnp.einsum("axp,anp->axn", weight, spec, preferred_element_type=jnp.float32)
    every_dx = every_dx.reshape(n_scol, n_dx, n_srow * n_dyl, 2 * k_blk * cols_here)
    dx_pick = dx_of_n[:, None, :, :] == jnp.arange(n_dx, dtype=jnp.int32)[None, :, None, None]
    summed = jnp.sum(jnp.where(dx_pick, every_dx, 0.0), axis=1)
    summed = summed.reshape(n_dev, 2 * n_dyl, k_blk * cols_here).astype(jnp.bfloat16)

    summed = lax.all_to_all(summed, ("scol", "srow"), split_axis=0, concat_axis=0, tiled=True)

    a_idx = lax.axis_index("scol")
    b_idx = lax.axis_index("srow")
    col_ids = jnp.arange(col_count, dtype=jnp.int32)
    my_j = b_idx * j_blk + jnp.arange(j_blk, dtype=jnp.int32)
    src_cos, src_sin = waves(jnp.arange(n_dev, dtype=jnp.int32) * cols_here, my_j, col_count)
    by_source = jnp.dot(
        summed.reshape(n_dev, -1).T.astype(jnp.float32),
        jnp.concatenate([src_cos, src_sin], axis=1),
        precision=lax.Precision.HIGH,
        preferred_element_type=jnp.float32,
    ).reshape(n_dyl, 2, k_blk, cols_here, 2, j_blk)
    part_re = by_source[:, 0, :, :, 0] + by_source[:, 1, :, :, 1]
    part_im = by_source[:, 1, :, :, 0] - by_source[:, 0, :, :, 1]
    tw_cos, tw_sin = waves(jnp.arange(cols_here, dtype=jnp.int32), my_j, col_count)
    tw_cos = tw_cos[None, None, :, :]
    tw_sin = tw_sin[None, None, :, :]
    per_shift_re = jnp.sum(part_re * tw_cos + part_im * tw_sin, axis=2)
    per_shift_im = jnp.sum(part_im * tw_cos - part_re * tw_sin, axis=2)
    my_start = jnp.array(dy_first, dtype=jnp.int32)[b_idx]
    pick = (shift_index(my_j, col_count) - 2 * RAD - my_start)[None, :] == jnp.arange(n_dyl, dtype=jnp.int32)[:, None]
    pick = pick[:, None, :]
    psi = jnp.stack(
        [
            jnp.sum(jnp.where(pick, per_shift_re, 0.0), axis=0),
            jnp.sum(jnp.where(pick, per_shift_im, 0.0), axis=0),
        ],
        axis=1,
    )

    my_k = a_idx * k_blk + jnp.arange(k_blk, dtype=jnp.int32)
    inv_cos, inv_sin = waves(row_ids, my_k, row_count)
    inverse_rows = jnp.concatenate(
        [
            jnp.concatenate([inv_cos, -inv_sin], axis=1),
            jnp.concatenate([inv_sin, inv_cos], axis=1),
        ],
        axis=0,
    )
    psi = psi.transpose(1, 0, 2).reshape(2 * k_blk, j_blk)
    half = jnp.dot(inverse_rows, psi, precision=lax.Precision.HIGH, preferred_element_type=jnp.float32)
    half = half.reshape(2, n_scol, row_count // n_scol, j_blk).transpose(1, 0, 2, 3)
    half = lax.all_to_all(half.astype(jnp.bfloat16), "scol", split_axis=0, concat_axis=0, tiled=True)
    half = jnp.sum(half.astype(jnp.float32), axis=0)
    out_rows = half.shape[1]

    out_cols = col_count // n_srow
    inv_cos, inv_sin = waves(my_j, col_ids, col_count)
    inverse_cols = jnp.concatenate(
        [
            jnp.concatenate([inv_cos, inv_sin], axis=1),
            jnp.concatenate([-inv_sin, inv_cos], axis=1),
        ],
        axis=0,
    )
    half = half.transpose(1, 0, 2).reshape(out_rows, 2 * j_blk)
    image = jnp.dot(half, inverse_cols, precision=lax.Precision.HIGH, preferred_element_type=jnp.float32)
    image = image.reshape(out_rows, 2, n_srow, out_cols).transpose(2, 0, 1, 3)
    image = lax.all_to_all(image.astype(jnp.bfloat16), "srow", split_axis=0, concat_axis=0, tiled=True)
    image = jnp.sum(image.astype(jnp.float32), axis=0) * (1.0 / (row_count * col_count))
    return image


def solution(mesh):
    placed = (P("srow", "scol", None), P(), P(), P())
    return jax.shard_map(
        on_device, mesh=mesh, in_specs=placed, out_specs=P("scol", None, "srow"), check_vma=False
    )
```

```python
import math

import jax
import jax.numpy as jnp
from jax import lax
from jax.sharding import PartitionSpec as P

DET = 32
RAD = 13
HIGHEST = lax.Precision.HIGHEST


def waves(left_ids, right_ids, length):
    product = left_ids[:, None] * right_ids[None, :] % length
    phases = product.astype(jnp.float32) * (2.0 * math.pi / length)
    return (jnp.cos(phases), jnp.sin(phases))


def square_waves(count):
    minor = min(128, count)
    ids = jnp.arange(count, dtype=jnp.int32)
    major_cos, major_sin = waves(ids, jnp.arange(count // minor, dtype=jnp.int32) * minor, count)
    minor_cos, minor_sin = waves(ids, jnp.arange(minor, dtype=jnp.int32), count)
    major_cos = jnp.repeat(major_cos, minor, axis=1)
    major_sin = jnp.repeat(major_sin, minor, axis=1)
    minor_cos = jnp.tile(minor_cos, (1, count // minor))
    minor_sin = jnp.tile(minor_sin, (1, count // minor))
    return (
        major_cos * minor_cos - major_sin * minor_sin,
        major_sin * minor_cos + major_cos * minor_sin,
    )


def shift_index(freq, count):
    signed = jnp.where(freq >= count // 2, freq - count, freq)
    return signed * (4 * RAD) // count + 2 * RAD


def split_dot(left, right):
    hi = lax.reduce_precision(left, exponent_bits=8, mantissa_bits=7)
    lo = left - hi
    return jnp.dot(hi.astype(jnp.bfloat16), right, preferred_element_type=jnp.float32) + jnp.dot(
        lo.astype(jnp.bfloat16), right, preferred_element_type=jnp.float32
    )


def on_device(frames, pixel_gain, eigen_flats, pixels):
    n_srow = lax.axis_size("srow")
    n_scol = lax.axis_size("scol")
    n_dev = n_srow * n_scol
    local_rows, local_cols, n_pix = frames.shape
    row_count = local_rows * n_srow
    col_count = local_cols * n_scol
    n_shift = 4 * RAD
    flat_index = lax.axis_index("scol") * n_srow + lax.axis_index("srow")

    readings = frames.astype(jnp.float32)
    exposure = jnp.mean(readings, axis=2, keepdims=True)
    gram = jnp.dot(eigen_flats.T, eigen_flats, precision=HIGHEST, preferred_element_type=jnp.float32)
    project = pixel_gain[:, None] * (jnp.eye(n_pix, dtype=jnp.float32) - gram)
    project_hi = lax.reduce_precision(project, exponent_bits=8, mantissa_bits=7)
    project_lo = (project - project_hi).astype(jnp.bfloat16)
    rows_in = frames.reshape(local_rows * local_cols, n_pix)
    corrected = jnp.dot(
        rows_in, project_hi.astype(jnp.bfloat16), preferred_element_type=jnp.float32
    ) + jnp.dot(rows_in, project_lo, preferred_element_type=jnp.float32)
    flattened = (corrected.reshape(local_rows, local_cols, n_pix) / exposure).astype(jnp.bfloat16)

    gathered = lax.all_to_all(flattened, "srow", split_axis=1, concat_axis=0, tiled=True)
    cols_here = gathered.shape[1]

    k_blk = row_count // n_scol
    j_blk = col_count // n_srow
    row_ids = jnp.arange(row_count, dtype=jnp.int32)
    row_cos, row_sin = square_waves(row_count)
    forward_rows = jnp.stack([row_cos, -row_sin], axis=0).reshape(2, n_scol, k_blk, row_count)
    forward_rows = forward_rows.transpose(1, 0, 2, 3).reshape(2 * row_count, row_count)
    spec = jnp.dot(
        forward_rows.astype(jnp.bfloat16),
        gathered.reshape(row_count, cols_here * n_pix),
        preferred_element_type=jnp.float32,
    ).astype(jnp.bfloat16)
    spec = spec.reshape(n_scol, 2 * k_blk * cols_here, n_pix)

    def shift_of(freq, count):
        signed = freq - count if freq >= count // 2 else freq
        return (signed * (4 * RAD)) // count

    dx_first, dy_first = [], []
    for a in range(n_scol):
        shifts = [shift_of(k, row_count) for k in range(a * k_blk, (a + 1) * k_blk)]
        dx_first.append(min(shifts))
    n_dx = max(
        max(shift_of(k, row_count) for k in range(a * k_blk, (a + 1) * k_blk)) - dx_first[a] + 1
        for a in range(n_scol)
    )
    for b in range(n_srow):
        dy_first.append(min(shift_of(j, col_count) for j in range(b * j_blk, (b + 1) * j_blk)))
    n_dyl = max(
        max(shift_of(j, col_count) for j in range(b * j_blk, (b + 1) * j_blk)) - dy_first[b] + 1
        for b in range(n_srow)
    )
    n_dyl = -(-n_dyl // 8) * 8
    move_x = (jnp.array(dx_first, dtype=jnp.int32)[:, None] + jnp.arange(n_dx, dtype=jnp.int32)[None, :])
    move_y = (jnp.array(dy_first, dtype=jnp.int32)[:, None] + jnp.arange(n_dyl, dtype=jnp.int32)[None, :])
    move_x = move_x[:, None, None, :, None]
    move_y = move_y[None, :, :, None, None]
    det_x = (pixels % DET - DET // 2)[None, None, None, None, :]
    det_y = (pixels // DET - DET // 2)[None, None, None, None, :]
    upper = (det_x - move_x) * (det_x - move_x) + (det_y - move_y) * (det_y - move_y) <= RAD * RAD
    lower = (det_x + move_x) * (det_x + move_x) + (det_y + move_y) * (det_y + move_y) <= RAD * RAD
    weight = (upper.astype(jnp.float32) - lower.astype(jnp.float32)).astype(jnp.bfloat16)
    own_dx = (shift_index(row_ids, row_count) - 2 * RAD).reshape(n_scol, k_blk)
    own_dx = own_dx - jnp.array(dx_first, dtype=jnp.int32)[:, None]
    dx_of_n = jnp.broadcast_to(own_dx[:, None, :, None], (n_scol, 2, k_blk, cols_here))
    dx_of_n = dx_of_n.reshape(n_scol, 1, 2 * k_blk * cols_here)
    weight = weight.transpose(0, 3, 1, 2, 4).reshape(n_scol, n_dx * n_srow * n_dyl, n_pix)
    every_dx = jnp.einsum("axp,anp->axn", weight, spec, preferred_element_type=jnp.float32)
    every_dx = every_dx.reshape(n_scol, n_dx, n_srow * n_dyl, 2 * k_blk * cols_here)
    dx_pick = dx_of_n[:, None, :, :] == jnp.arange(n_dx, dtype=jnp.int32)[None, :, None, None]
    summed = jnp.sum(jnp.where(dx_pick, every_dx, 0.0), axis=1)
    summed = summed.reshape(n_dev, n_dyl, 2 * k_blk * cols_here).astype(jnp.bfloat16)

    summed = lax.all_to_all(summed, ("scol", "srow"), split_axis=0, concat_axis=0, tiled=True)

    a_idx = lax.axis_index("scol")
    b_idx = lax.axis_index("srow")
    col_ids = jnp.arange(col_count, dtype=jnp.int32)
    my_j = b_idx * j_blk + jnp.arange(j_blk, dtype=jnp.int32)
    src_cos, src_sin = waves(jnp.arange(n_dev, dtype=jnp.int32) * cols_here, my_j, col_count)
    by_source = jnp.dot(
        summed.reshape(n_dev, -1).T.astype(jnp.float32),
        jnp.concatenate([src_cos, src_sin], axis=1),
        precision=lax.Precision.HIGH,
        preferred_element_type=jnp.float32,
    ).reshape(n_dyl, 2, k_blk, cols_here, 2, j_blk)
    part_re = by_source[:, 0, :, :, 0] + by_source[:, 1, :, :, 1]
    part_im = by_source[:, 1, :, :, 0] - by_source[:, 0, :, :, 1]
    tw_cos, tw_sin = waves(jnp.arange(cols_here, dtype=jnp.int32), my_j, col_count)
    tw_cos = tw_cos[None, None, :, :]
    tw_sin = tw_sin[None, None, :, :]
    per_shift_re = jnp.sum(part_re * tw_cos + part_im * tw_sin, axis=2)
    per_shift_im = jnp.sum(part_im * tw_cos - part_re * tw_sin, axis=2)
    my_start = jnp.array(dy_first, dtype=jnp.int32)[b_idx]
    pick = (shift_index(my_j, col_count) - 2 * RAD - my_start)[None, :] == jnp.arange(n_dyl, dtype=jnp.int32)[:, None]
    pick = pick[:, None, :]
    psi = jnp.stack(
        [
            jnp.sum(jnp.where(pick, per_shift_re, 0.0), axis=0),
            jnp.sum(jnp.where(pick, per_shift_im, 0.0), axis=0),
        ],
        axis=1,
    )

    my_k = a_idx * k_blk + jnp.arange(k_blk, dtype=jnp.int32)
    inv_cos, inv_sin = waves(row_ids, my_k, row_count)
    inverse_rows = jnp.concatenate(
        [
            jnp.concatenate([inv_cos, -inv_sin], axis=1),
            jnp.concatenate([inv_sin, inv_cos], axis=1),
        ],
        axis=0,
    )
    psi = psi.transpose(1, 0, 2).reshape(2 * k_blk, j_blk)
    half = jnp.dot(inverse_rows, psi, precision=lax.Precision.HIGH, preferred_element_type=jnp.float32)
    half = half.reshape(2, n_scol, row_count // n_scol, j_blk).transpose(1, 0, 2, 3)
    half = lax.all_to_all(half.astype(jnp.bfloat16), "scol", split_axis=0, concat_axis=0, tiled=True)
    half = jnp.sum(half.astype(jnp.float32), axis=0)
    out_rows = half.shape[1]

    out_cols = col_count // n_srow
    inv_cos, inv_sin = waves(my_j, col_ids, col_count)
    inverse_cols = jnp.concatenate(
        [
            jnp.concatenate([inv_cos, inv_sin], axis=1),
            jnp.concatenate([-inv_sin, inv_cos], axis=1),
        ],
        axis=0,
    )
    half = half.transpose(1, 0, 2).reshape(out_rows, 2 * j_blk)
    image = jnp.dot(half, inverse_cols, precision=lax.Precision.HIGH, preferred_element_type=jnp.float32)
    image = image.reshape(out_rows, 2, n_srow, out_cols).transpose(2, 0, 1, 3)
    image = lax.all_to_all(image.astype(jnp.bfloat16), "srow", split_axis=0, concat_axis=0, tiled=True)
    image = jnp.sum(image.astype(jnp.float32), axis=0) * (1.0 / (row_count * col_count))
    return image


def solution(mesh):
    placed = (P("srow", "scol", None), P(), P(), P())
    return jax.shard_map(
        on_device, mesh=mesh, in_specs=placed, out_specs=P("scol", None, "srow"), check_vma=False
    )
```

```python
import math

import jax
import jax.numpy as jnp
from jax import lax
from jax.sharding import PartitionSpec as P

DET = 32
RAD = 13
HIGHEST = lax.Precision.HIGHEST


def waves(left_ids, right_ids, length):
    product = left_ids[:, None] * right_ids[None, :] % length
    phases = product.astype(jnp.float32) * (2.0 * math.pi / length)
    return (jnp.cos(phases), jnp.sin(phases))


def square_waves(count):
    minor = min(128, count)
    ids = jnp.arange(count, dtype=jnp.int32)
    major_cos, major_sin = waves(ids, jnp.arange(count // minor, dtype=jnp.int32) * minor, count)
    minor_cos, minor_sin = waves(ids, jnp.arange(minor, dtype=jnp.int32), count)
    major_cos = jnp.repeat(major_cos, minor, axis=1)
    major_sin = jnp.repeat(major_sin, minor, axis=1)
    minor_cos = jnp.tile(minor_cos, (1, count // minor))
    minor_sin = jnp.tile(minor_sin, (1, count // minor))
    return (
        major_cos * minor_cos - major_sin * minor_sin,
        major_sin * minor_cos + major_cos * minor_sin,
    )


def shift_index(freq, count):
    signed = jnp.where(freq >= count // 2, freq - count, freq)
    return signed * (4 * RAD) // count + 2 * RAD


def split_dot(left, right):
    hi = lax.reduce_precision(left, exponent_bits=8, mantissa_bits=7)
    lo = left - hi
    return jnp.dot(hi.astype(jnp.bfloat16), right, preferred_element_type=jnp.float32) + jnp.dot(
        lo.astype(jnp.bfloat16), right, preferred_element_type=jnp.float32
    )


def on_device(frames, pixel_gain, eigen_flats, pixels):
    n_srow = lax.axis_size("srow")
    n_scol = lax.axis_size("scol")
    n_dev = n_srow * n_scol
    local_rows, local_cols, n_pix = frames.shape
    row_count = local_rows * n_srow
    col_count = local_cols * n_scol
    n_shift = 4 * RAD
    flat_index = lax.axis_index("scol") * n_srow + lax.axis_index("srow")

    readings = frames.astype(jnp.float32)
    exposure = jnp.mean(readings, axis=2, keepdims=True)
    gram = jnp.dot(eigen_flats.T, eigen_flats, precision=HIGHEST, preferred_element_type=jnp.float32)
    project = pixel_gain[:, None] * (jnp.eye(n_pix, dtype=jnp.float32) - gram)
    corrected = jnp.einsum("rcp,pq->rcq", readings, project, precision=lax.Precision.HIGH)
    flattened = (corrected / exposure).astype(jnp.bfloat16)

    gathered = lax.all_to_all(flattened, "srow", split_axis=1, concat_axis=0, tiled=True)
    cols_here = gathered.shape[1]

    k_blk = row_count // n_scol
    j_blk = col_count // n_srow
    row_ids = jnp.arange(row_count, dtype=jnp.int32)
    row_cos, row_sin = square_waves(row_count)
    forward_rows = jnp.stack([row_cos, -row_sin], axis=0).reshape(2, n_scol, k_blk, row_count)
    forward_rows = forward_rows.transpose(1, 0, 2, 3).reshape(2 * row_count, row_count)
    spec = jnp.dot(
        forward_rows.astype(jnp.bfloat16),
        gathered.reshape(row_count, cols_here * n_pix),
        preferred_element_type=jnp.float32,
    ).astype(jnp.bfloat16)
    spec = spec.reshape(n_scol, 2 * k_blk * cols_here, n_pix)

    def shift_of(freq, count):
        signed = freq - count if freq >= count // 2 else freq
        return (signed * (4 * RAD)) // count

    dx_first, dy_first = [], []
    for a in range(n_scol):
        shifts = [shift_of(k, row_count) for k in range(a * k_blk, (a + 1) * k_blk)]
        dx_first.append(min(shifts))
    n_dx = max(
        max(shift_of(k, row_count) for k in range(a * k_blk, (a + 1) * k_blk)) - dx_first[a] + 1
        for a in range(n_scol)
    )
    for b in range(n_srow):
        dy_first.append(min(shift_of(j, col_count) for j in range(b * j_blk, (b + 1) * j_blk)))
    n_dyl = max(
        max(shift_of(j, col_count) for j in range(b * j_blk, (b + 1) * j_blk)) - dy_first[b] + 1
        for b in range(n_srow)
    )
    n_dyl = -(-n_dyl // 8) * 8
    move_x = (jnp.array(dx_first, dtype=jnp.int32)[:, None] + jnp.arange(n_dx, dtype=jnp.int32)[None, :])
    move_y = (jnp.array(dy_first, dtype=jnp.int32)[:, None] + jnp.arange(n_dyl, dtype=jnp.int32)[None, :])
    move_x = move_x[:, None, None, :, None]
    move_y = move_y[None, :, :, None, None]
    det_x = (pixels % DET - DET // 2)[None, None, None, None, :]
    det_y = (pixels // DET - DET // 2)[None, None, None, None, :]
    upper = (det_x - move_x) * (det_x - move_x) + (det_y - move_y) * (det_y - move_y) <= RAD * RAD
    lower = (det_x + move_x) * (det_x + move_x) + (det_y + move_y) * (det_y + move_y) <= RAD * RAD
    weight = (upper.astype(jnp.float32) - lower.astype(jnp.float32)).astype(jnp.bfloat16)
    own_dx = (shift_index(row_ids, row_count) - 2 * RAD).reshape(n_scol, k_blk)
    own_dx = own_dx - jnp.array(dx_first, dtype=jnp.int32)[:, None]
    dx_of_n = jnp.broadcast_to(own_dx[:, None, :, None], (n_scol, 2, k_blk, cols_here))
    dx_of_n = dx_of_n.reshape(n_scol, 1, 2 * k_blk * cols_here)
    weight = weight.transpose(0, 3, 1, 2, 4).reshape(n_scol, n_dx * n_srow * n_dyl, n_pix)
    every_dx = jnp.einsum("axp,anp->axn", weight, spec, preferred_element_type=jnp.float32)
    every_dx = every_dx.reshape(n_scol, n_dx, n_srow * n_dyl, 2 * k_blk * cols_here)
    dx_pick = dx_of_n[:, None, :, :] == jnp.arange(n_dx, dtype=jnp.int32)[None, :, None, None]
    summed = jnp.sum(jnp.where(dx_pick, every_dx, 0.0), axis=1)
    summed = summed.reshape(n_dev, n_dyl, 2 * k_blk * cols_here).astype(jnp.bfloat16)

    summed = lax.all_to_all(summed, ("scol", "srow"), split_axis=0, concat_axis=0, tiled=True)

    a_idx = lax.axis_index("scol")
    b_idx = lax.axis_index("srow")
    col_ids = jnp.arange(col_count, dtype=jnp.int32)
    my_j = b_idx * j_blk + jnp.arange(j_blk, dtype=jnp.int32)
    src_cos, src_sin = waves(jnp.arange(n_dev, dtype=jnp.int32) * cols_here, my_j, col_count)
    by_source = jnp.dot(
        summed.reshape(n_dev, -1).T.astype(jnp.float32),
        jnp.concatenate([src_cos, src_sin], axis=1),
        precision=lax.Precision.HIGH,
        preferred_element_type=jnp.float32,
    ).reshape(n_dyl, 2, k_blk, cols_here, 2, j_blk)
    part_re = by_source[:, 0, :, :, 0] + by_source[:, 1, :, :, 1]
    part_im = by_source[:, 1, :, :, 0] - by_source[:, 0, :, :, 1]
    tw_cos, tw_sin = waves(jnp.arange(cols_here, dtype=jnp.int32), my_j, col_count)
    tw_cos = tw_cos[None, None, :, :]
    tw_sin = tw_sin[None, None, :, :]
    per_shift_re = jnp.sum(part_re * tw_cos + part_im * tw_sin, axis=2)
    per_shift_im = jnp.sum(part_im * tw_cos - part_re * tw_sin, axis=2)
    my_start = jnp.array(dy_first, dtype=jnp.int32)[b_idx]
    pick = (shift_index(my_j, col_count) - 2 * RAD - my_start)[None, :] == jnp.arange(n_dyl, dtype=jnp.int32)[:, None]
    pick = pick[:, None, :]
    psi = jnp.stack(
        [
            jnp.sum(jnp.where(pick, per_shift_re, 0.0), axis=0),
            jnp.sum(jnp.where(pick, per_shift_im, 0.0), axis=0),
        ],
        axis=1,
    )

    my_k = a_idx * k_blk + jnp.arange(k_blk, dtype=jnp.int32)
    inv_cos, inv_sin = waves(row_ids, my_k, row_count)
    inverse_rows = jnp.concatenate(
        [
            jnp.concatenate([inv_cos, -inv_sin], axis=1),
            jnp.concatenate([inv_sin, inv_cos], axis=1),
        ],
        axis=0,
    )
    psi = psi.transpose(1, 0, 2).reshape(2 * k_blk, j_blk)
    half = jnp.dot(inverse_rows, psi, precision=lax.Precision.HIGH, preferred_element_type=jnp.float32)
    half = half.reshape(2, n_scol, row_count // n_scol, j_blk).transpose(1, 0, 2, 3)
    half = lax.all_to_all(half.astype(jnp.bfloat16), "scol", split_axis=0, concat_axis=0, tiled=True)
    half = jnp.sum(half.astype(jnp.float32), axis=0)
    out_rows = half.shape[1]

    out_cols = col_count // n_srow
    inv_cos, inv_sin = waves(my_j, col_ids, col_count)
    inverse_cols = jnp.concatenate(
        [
            jnp.concatenate([inv_cos, inv_sin], axis=1),
            jnp.concatenate([-inv_sin, inv_cos], axis=1),
        ],
        axis=0,
    )
    half = half.transpose(1, 0, 2).reshape(out_rows, 2 * j_blk)
    image = jnp.dot(half, inverse_cols, precision=lax.Precision.HIGH, preferred_element_type=jnp.float32)
    image = image.reshape(out_rows, 2, n_srow, out_cols).transpose(2, 0, 1, 3)
    image = lax.all_to_all(image.astype(jnp.bfloat16), "srow", split_axis=0, concat_axis=0, tiled=True)
    image = jnp.sum(image.astype(jnp.float32), axis=0) * (1.0 / (row_count * col_count))
    return image


def solution(mesh):
    placed = (P("srow", "scol", None), P(), P(), P())
    return jax.shard_map(
        on_device, mesh=mesh, in_specs=placed, out_specs=P("scol", None, "srow"), check_vma=False
    )
```

```python
import math

import jax
import jax.numpy as jnp
from jax import lax
from jax.sharding import PartitionSpec as P

DET = 32
RAD = 13
HIGHEST = lax.Precision.HIGHEST


def waves(left_ids, right_ids, length):
    product = left_ids[:, None] * right_ids[None, :] % length
    phases = product.astype(jnp.float32) * (2.0 * math.pi / length)
    return (jnp.cos(phases), jnp.sin(phases))


def square_waves(count):
    minor = min(128, count)
    ids = jnp.arange(count, dtype=jnp.int32)
    major_cos, major_sin = waves(ids, jnp.arange(count // minor, dtype=jnp.int32) * minor, count)
    minor_cos, minor_sin = waves(ids, jnp.arange(minor, dtype=jnp.int32), count)
    major_cos = jnp.repeat(major_cos, minor, axis=1)
    major_sin = jnp.repeat(major_sin, minor, axis=1)
    minor_cos = jnp.tile(minor_cos, (1, count // minor))
    minor_sin = jnp.tile(minor_sin, (1, count // minor))
    return (
        major_cos * minor_cos - major_sin * minor_sin,
        major_sin * minor_cos + major_cos * minor_sin,
    )


def shift_index(freq, count):
    signed = jnp.where(freq >= count // 2, freq - count, freq)
    return signed * (4 * RAD) // count + 2 * RAD


def split_dot(left, right):
    hi = lax.reduce_precision(left, exponent_bits=8, mantissa_bits=7)
    lo = left - hi
    return jnp.dot(hi.astype(jnp.bfloat16), right, preferred_element_type=jnp.float32) + jnp.dot(
        lo.astype(jnp.bfloat16), right, preferred_element_type=jnp.float32
    )


def on_device(frames, pixel_gain, eigen_flats, pixels):
    n_srow = lax.axis_size("srow")
    n_scol = lax.axis_size("scol")
    n_dev = n_srow * n_scol
    local_rows, local_cols, n_pix = frames.shape
    row_count = local_rows * n_srow
    col_count = local_cols * n_scol
    n_shift = 4 * RAD
    flat_index = lax.axis_index("scol") * n_srow + lax.axis_index("srow")

    readings = frames.astype(jnp.float32)
    averaging = jnp.full((n_pix, 128), 1.0 / n_pix, dtype=jnp.bfloat16)
    exposure = jnp.einsum("rcp,pq->rcq", frames, averaging, preferred_element_type=jnp.float32)[:, :, :1]
    gram = jnp.dot(eigen_flats.T, eigen_flats, precision=HIGHEST, preferred_element_type=jnp.float32)
    project = pixel_gain[:, None] * (jnp.eye(n_pix, dtype=jnp.float32) - gram)
    corrected = jnp.einsum("rcp,pq->rcq", readings, project, precision=lax.Precision.HIGH)
    flattened = (corrected / exposure).astype(jnp.bfloat16)

    gathered = lax.all_to_all(flattened, "srow", split_axis=1, concat_axis=0, tiled=True)
    cols_here = gathered.shape[1]

    k_blk = row_count // n_scol
    j_blk = col_count // n_srow
    row_ids = jnp.arange(row_count, dtype=jnp.int32)
    row_cos, row_sin = square_waves(row_count)
    forward_rows = jnp.stack([row_cos, -row_sin], axis=0).reshape(2, n_scol, k_blk, row_count)
    forward_rows = forward_rows.transpose(1, 0, 2, 3).reshape(2 * row_count, row_count)
    spec = jnp.dot(
        forward_rows.astype(jnp.bfloat16),
        gathered.reshape(row_count, cols_here * n_pix),
        preferred_element_type=jnp.float32,
    ).astype(jnp.bfloat16)
    spec = spec.reshape(n_scol, 2 * k_blk * cols_here, n_pix)

    def shift_of(freq, count):
        signed = freq - count if freq >= count // 2 else freq
        return (signed * (4 * RAD)) // count

    dx_first, dy_first = [], []
    for a in range(n_scol):
        shifts = [shift_of(k, row_count) for k in range(a * k_blk, (a + 1) * k_blk)]
        dx_first.append(min(shifts))
    n_dx = max(
        max(shift_of(k, row_count) for k in range(a * k_blk, (a + 1) * k_blk)) - dx_first[a] + 1
        for a in range(n_scol)
    )
    for b in range(n_srow):
        dy_first.append(min(shift_of(j, col_count) for j in range(b * j_blk, (b + 1) * j_blk)))
    n_dyl = max(
        max(shift_of(j, col_count) for j in range(b * j_blk, (b + 1) * j_blk)) - dy_first[b] + 1
        for b in range(n_srow)
    )
    n_dyl = -(-n_dyl // 8) * 8
    move_x = (jnp.array(dx_first, dtype=jnp.int32)[:, None] + jnp.arange(n_dx, dtype=jnp.int32)[None, :])
    move_y = (jnp.array(dy_first, dtype=jnp.int32)[:, None] + jnp.arange(n_dyl, dtype=jnp.int32)[None, :])
    move_x = move_x[:, None, None, :, None]
    move_y = move_y[None, :, :, None, None]
    det_x = (pixels % DET - DET // 2)[None, None, None, None, :]
    det_y = (pixels // DET - DET // 2)[None, None, None, None, :]
    upper = (det_x - move_x) * (det_x - move_x) + (det_y - move_y) * (det_y - move_y) <= RAD * RAD
    lower = (det_x + move_x) * (det_x + move_x) + (det_y + move_y) * (det_y + move_y) <= RAD * RAD
    weight = (upper.astype(jnp.float32) - lower.astype(jnp.float32)).astype(jnp.bfloat16)
    own_dx = (shift_index(row_ids, row_count) - 2 * RAD).reshape(n_scol, k_blk)
    own_dx = own_dx - jnp.array(dx_first, dtype=jnp.int32)[:, None]
    dx_of_n = jnp.broadcast_to(own_dx[:, None, :, None], (n_scol, 2, k_blk, cols_here))
    dx_of_n = dx_of_n.reshape(n_scol, 1, 2 * k_blk * cols_here)
    weight = weight.transpose(0, 3, 1, 2, 4).reshape(n_scol, n_dx * n_srow * n_dyl, n_pix)
    every_dx = jnp.einsum("axp,anp->axn", weight, spec, preferred_element_type=jnp.float32)
    every_dx = every_dx.reshape(n_scol, n_dx, n_srow * n_dyl, 2 * k_blk * cols_here)
    dx_pick = dx_of_n[:, None, :, :] == jnp.arange(n_dx, dtype=jnp.int32)[None, :, None, None]
    summed = jnp.sum(jnp.where(dx_pick, every_dx, 0.0), axis=1)
    summed = summed.reshape(n_dev, n_dyl, 2 * k_blk * cols_here).astype(jnp.bfloat16)

    summed = lax.all_to_all(summed, ("scol", "srow"), split_axis=0, concat_axis=0, tiled=True)

    a_idx = lax.axis_index("scol")
    b_idx = lax.axis_index("srow")
    col_ids = jnp.arange(col_count, dtype=jnp.int32)
    my_j = b_idx * j_blk + jnp.arange(j_blk, dtype=jnp.int32)
    src_cos, src_sin = waves(jnp.arange(n_dev, dtype=jnp.int32) * cols_here, my_j, col_count)
    by_source = jnp.dot(
        summed.reshape(n_dev, -1).T.astype(jnp.float32),
        jnp.concatenate([src_cos, src_sin], axis=1),
        precision=lax.Precision.HIGH,
        preferred_element_type=jnp.float32,
    ).reshape(n_dyl, 2, k_blk, cols_here, 2, j_blk)
    part_re = by_source[:, 0, :, :, 0] + by_source[:, 1, :, :, 1]
    part_im = by_source[:, 1, :, :, 0] - by_source[:, 0, :, :, 1]
    tw_cos, tw_sin = waves(jnp.arange(cols_here, dtype=jnp.int32), my_j, col_count)
    tw_cos = tw_cos[None, None, :, :]
    tw_sin = tw_sin[None, None, :, :]
    per_shift_re = jnp.sum(part_re * tw_cos + part_im * tw_sin, axis=2)
    per_shift_im = jnp.sum(part_im * tw_cos - part_re * tw_sin, axis=2)
    my_start = jnp.array(dy_first, dtype=jnp.int32)[b_idx]
    pick = (shift_index(my_j, col_count) - 2 * RAD - my_start)[None, :] == jnp.arange(n_dyl, dtype=jnp.int32)[:, None]
    pick = pick[:, None, :]
    psi = jnp.stack(
        [
            jnp.sum(jnp.where(pick, per_shift_re, 0.0), axis=0),
            jnp.sum(jnp.where(pick, per_shift_im, 0.0), axis=0),
        ],
        axis=1,
    )

    my_k = a_idx * k_blk + jnp.arange(k_blk, dtype=jnp.int32)
    inv_cos, inv_sin = waves(row_ids, my_k, row_count)
    inverse_rows = jnp.concatenate(
        [
            jnp.concatenate([inv_cos, -inv_sin], axis=1),
            jnp.concatenate([inv_sin, inv_cos], axis=1),
        ],
        axis=0,
    )
    psi = psi.transpose(1, 0, 2).reshape(2 * k_blk, j_blk)
    half = jnp.dot(inverse_rows, psi, precision=lax.Precision.HIGH, preferred_element_type=jnp.float32)
    half = half.reshape(2, n_scol, row_count // n_scol, j_blk).transpose(1, 0, 2, 3)
    half = lax.all_to_all(half.astype(jnp.bfloat16), "scol", split_axis=0, concat_axis=0, tiled=True)
    half = jnp.sum(half.astype(jnp.float32), axis=0)
    out_rows = half.shape[1]

    out_cols = col_count // n_srow
    inv_cos, inv_sin = waves(my_j, col_ids, col_count)
    inverse_cols = jnp.concatenate(
        [
            jnp.concatenate([inv_cos, inv_sin], axis=1),
            jnp.concatenate([-inv_sin, inv_cos], axis=1),
        ],
        axis=0,
    )
    half = half.transpose(1, 0, 2).reshape(out_rows, 2 * j_blk)
    image = jnp.dot(half, inverse_cols, precision=lax.Precision.HIGH, preferred_element_type=jnp.float32)
    image = image.reshape(out_rows, 2, n_srow, out_cols).transpose(2, 0, 1, 3)
    image = lax.all_to_all(image.astype(jnp.bfloat16), "srow", split_axis=0, concat_axis=0, tiled=True)
    image = jnp.sum(image.astype(jnp.float32), axis=0) * (1.0 / (row_count * col_count))
    return image


def solution(mesh):
    placed = (P("srow", "scol", None), P(), P(), P())
    return jax.shard_map(
        on_device, mesh=mesh, in_specs=placed, out_specs=P("scol", None, "srow"), check_vma=False
    )
```

```python
import math

import jax
import jax.numpy as jnp
from jax import lax
from jax.sharding import PartitionSpec as P

DET = 32
RAD = 13
HIGHEST = lax.Precision.HIGHEST


def waves(left_ids, right_ids, length):
    product = left_ids[:, None] * right_ids[None, :] % length
    phases = product.astype(jnp.float32) * (2.0 * math.pi / length)
    return (jnp.cos(phases), jnp.sin(phases))


def square_waves(count):
    minor = min(128, count)
    ids = jnp.arange(count, dtype=jnp.int32)
    major_cos, major_sin = waves(ids, jnp.arange(count // minor, dtype=jnp.int32) * minor, count)
    minor_cos, minor_sin = waves(ids, jnp.arange(minor, dtype=jnp.int32), count)
    major_cos = jnp.repeat(major_cos, minor, axis=1)
    major_sin = jnp.repeat(major_sin, minor, axis=1)
    minor_cos = jnp.tile(minor_cos, (1, count // minor))
    minor_sin = jnp.tile(minor_sin, (1, count // minor))
    return (
        major_cos * minor_cos - major_sin * minor_sin,
        major_sin * minor_cos + major_cos * minor_sin,
    )


def shift_index(freq, count):
    signed = jnp.where(freq >= count // 2, freq - count, freq)
    return signed * (4 * RAD) // count + 2 * RAD


def split_dot(left, right):
    hi = lax.reduce_precision(left, exponent_bits=8, mantissa_bits=7)
    lo = left - hi
    return jnp.dot(hi.astype(jnp.bfloat16), right, preferred_element_type=jnp.float32) + jnp.dot(
        lo.astype(jnp.bfloat16), right, preferred_element_type=jnp.float32
    )


def on_device(frames, pixel_gain, eigen_flats, pixels):
    n_srow = lax.axis_size("srow")
    n_scol = lax.axis_size("scol")
    n_dev = n_srow * n_scol
    local_rows, local_cols, n_pix = frames.shape
    row_count = local_rows * n_srow
    col_count = local_cols * n_scol
    n_shift = 4 * RAD
    flat_index = lax.axis_index("scol") * n_srow + lax.axis_index("srow")

    readings = frames.astype(jnp.float32)
    exposure = jnp.mean(readings, axis=2, keepdims=True)
    gram = jnp.dot(eigen_flats.T, eigen_flats, precision=HIGHEST, preferred_element_type=jnp.float32)
    project = pixel_gain[:, None] * (jnp.eye(n_pix, dtype=jnp.float32) - gram)
    corrected = jnp.einsum("rcp,pq->rcq", readings, project, precision=lax.Precision.HIGH)
    flattened = (corrected / exposure).astype(jnp.bfloat16)

    gathered = lax.all_to_all(flattened, "srow", split_axis=1, concat_axis=0, tiled=True)
    cols_here = gathered.shape[1]

    k_blk = row_count // n_scol
    j_blk = col_count // n_srow
    row_ids = jnp.arange(row_count, dtype=jnp.int32)
    row_cos, row_sin = square_waves(row_count)
    forward_rows = jnp.stack([row_cos, -row_sin], axis=0).reshape(2, n_scol, k_blk, row_count)
    forward_rows = forward_rows.transpose(1, 0, 2, 3).reshape(2 * row_count, row_count)
    spec = jnp.dot(
        forward_rows.astype(jnp.bfloat16),
        gathered.reshape(row_count, cols_here * n_pix),
        preferred_element_type=jnp.float32,
    ).astype(jnp.bfloat16)
    spec = spec.reshape(n_scol, 2 * k_blk * cols_here, n_pix)

    def shift_of(freq, count):
        signed = freq - count if freq >= count // 2 else freq
        return (signed * (4 * RAD)) // count

    dx_first, dy_first = [], []
    for a in range(n_scol):
        shifts = [shift_of(k, row_count) for k in range(a * k_blk, (a + 1) * k_blk)]
        dx_first.append(min(shifts))
    n_dx = max(
        max(shift_of(k, row_count) for k in range(a * k_blk, (a + 1) * k_blk)) - dx_first[a] + 1
        for a in range(n_scol)
    )
    for b in range(n_srow):
        dy_first.append(min(shift_of(j, col_count) for j in range(b * j_blk, (b + 1) * j_blk)))
    n_dyl = max(
        max(shift_of(j, col_count) for j in range(b * j_blk, (b + 1) * j_blk)) - dy_first[b] + 1
        for b in range(n_srow)
    )
    n_dyl = -(-n_dyl // 8) * 8
    move_x = (jnp.array(dx_first, dtype=jnp.int32)[:, None] + jnp.arange(n_dx, dtype=jnp.int32)[None, :])
    move_y = (jnp.array(dy_first, dtype=jnp.int32)[:, None] + jnp.arange(n_dyl, dtype=jnp.int32)[None, :])
    move_x = move_x[:, None, None, :, None]
    move_y = move_y[None, :, :, None, None]
    det_x = (pixels % DET - DET // 2)[None, None, None, None, :]
    det_y = (pixels // DET - DET // 2)[None, None, None, None, :]
    upper = (det_x - move_x) * (det_x - move_x) + (det_y - move_y) * (det_y - move_y) <= RAD * RAD
    lower = (det_x + move_x) * (det_x + move_x) + (det_y + move_y) * (det_y + move_y) <= RAD * RAD
    weight = (upper.astype(jnp.float32) - lower.astype(jnp.float32)).astype(jnp.bfloat16)
    own_dx = (shift_index(row_ids, row_count) - 2 * RAD).reshape(n_scol, k_blk)
    own_dx = own_dx - jnp.array(dx_first, dtype=jnp.int32)[:, None]
    dx_of_n = jnp.broadcast_to(own_dx[:, None, :, None], (n_scol, 2, k_blk, cols_here))
    dx_of_n = dx_of_n.reshape(n_scol, 1, 2 * k_blk * cols_here)
    weight = weight.transpose(0, 3, 1, 2, 4).reshape(n_scol, n_dx * n_srow * n_dyl, n_pix)
    every_dx = jnp.einsum("axp,anp->axn", weight, spec, preferred_element_type=jnp.bfloat16)
    every_dx = every_dx.reshape(n_scol, n_dx, n_srow * n_dyl, 2 * k_blk * cols_here)
    dx_pick = dx_of_n[:, None, :, :] == jnp.arange(n_dx, dtype=jnp.int32)[None, :, None, None]
    summed = jnp.sum(jnp.where(dx_pick, every_dx, jnp.zeros((), jnp.bfloat16)), axis=1)
    summed = summed.reshape(n_dev, n_dyl, 2 * k_blk * cols_here).astype(jnp.bfloat16)

    summed = lax.all_to_all(summed, ("scol", "srow"), split_axis=0, concat_axis=0, tiled=True)

    a_idx = lax.axis_index("scol")
    b_idx = lax.axis_index("srow")
    col_ids = jnp.arange(col_count, dtype=jnp.int32)
    my_j = b_idx * j_blk + jnp.arange(j_blk, dtype=jnp.int32)
    src_cos, src_sin = waves(jnp.arange(n_dev, dtype=jnp.int32) * cols_here, my_j, col_count)
    by_source = jnp.dot(
        summed.reshape(n_dev, -1).T.astype(jnp.float32),
        jnp.concatenate([src_cos, src_sin], axis=1),
        precision=lax.Precision.HIGH,
        preferred_element_type=jnp.float32,
    ).reshape(n_dyl, 2, k_blk, cols_here, 2, j_blk)
    part_re = by_source[:, 0, :, :, 0] + by_source[:, 1, :, :, 1]
    part_im = by_source[:, 1, :, :, 0] - by_source[:, 0, :, :, 1]
    tw_cos, tw_sin = waves(jnp.arange(cols_here, dtype=jnp.int32), my_j, col_count)
    tw_cos = tw_cos[None, None, :, :]
    tw_sin = tw_sin[None, None, :, :]
    per_shift_re = jnp.sum(part_re * tw_cos + part_im * tw_sin, axis=2)
    per_shift_im = jnp.sum(part_im * tw_cos - part_re * tw_sin, axis=2)
    my_start = jnp.array(dy_first, dtype=jnp.int32)[b_idx]
    pick = (shift_index(my_j, col_count) - 2 * RAD - my_start)[None, :] == jnp.arange(n_dyl, dtype=jnp.int32)[:, None]
    pick = pick[:, None, :]
    psi = jnp.stack(
        [
            jnp.sum(jnp.where(pick, per_shift_re, 0.0), axis=0),
            jnp.sum(jnp.where(pick, per_shift_im, 0.0), axis=0),
        ],
        axis=1,
    )

    my_k = a_idx * k_blk + jnp.arange(k_blk, dtype=jnp.int32)
    inv_cos, inv_sin = waves(row_ids, my_k, row_count)
    inverse_rows = jnp.concatenate(
        [
            jnp.concatenate([inv_cos, -inv_sin], axis=1),
            jnp.concatenate([inv_sin, inv_cos], axis=1),
        ],
        axis=0,
    )
    psi = psi.transpose(1, 0, 2).reshape(2 * k_blk, j_blk)
    half = jnp.dot(inverse_rows, psi, precision=lax.Precision.HIGH, preferred_element_type=jnp.float32)
    half = half.reshape(2, n_scol, row_count // n_scol, j_blk).transpose(1, 0, 2, 3)
    half = lax.all_to_all(half.astype(jnp.bfloat16), "scol", split_axis=0, concat_axis=0, tiled=True)
    half = jnp.sum(half.astype(jnp.float32), axis=0)
    out_rows = half.shape[1]

    out_cols = col_count // n_srow
    inv_cos, inv_sin = waves(my_j, col_ids, col_count)
    inverse_cols = jnp.concatenate(
        [
            jnp.concatenate([inv_cos, inv_sin], axis=1),
            jnp.concatenate([-inv_sin, inv_cos], axis=1),
        ],
        axis=0,
    )
    half = half.transpose(1, 0, 2).reshape(out_rows, 2 * j_blk)
    image = jnp.dot(half, inverse_cols, precision=lax.Precision.HIGH, preferred_element_type=jnp.float32)
    image = image.reshape(out_rows, 2, n_srow, out_cols).transpose(2, 0, 1, 3)
    image = lax.all_to_all(image.astype(jnp.bfloat16), "srow", split_axis=0, concat_axis=0, tiled=True)
    image = jnp.sum(image.astype(jnp.float32), axis=0) * (1.0 / (row_count * col_count))
    return image


def solution(mesh):
    placed = (P("srow", "scol", None), P(), P(), P())
    return jax.shard_map(
        on_device, mesh=mesh, in_specs=placed, out_specs=P("scol", None, "srow"), check_vma=False
    )
```

```python
import math

import jax
import jax.numpy as jnp
from jax import lax
from jax.sharding import PartitionSpec as P

DET = 32
RAD = 13
HIGHEST = lax.Precision.HIGHEST


def waves(left_ids, right_ids, length):
    product = left_ids[:, None] * right_ids[None, :] % length
    phases = product.astype(jnp.float32) * (2.0 * math.pi / length)
    return (jnp.cos(phases), jnp.sin(phases))


def square_waves(count):
    minor = min(128, count)
    ids = jnp.arange(count, dtype=jnp.int32)
    major_cos, major_sin = waves(ids, jnp.arange(count // minor, dtype=jnp.int32) * minor, count)
    minor_cos, minor_sin = waves(ids, jnp.arange(minor, dtype=jnp.int32), count)
    major_cos = jnp.repeat(major_cos, minor, axis=1)
    major_sin = jnp.repeat(major_sin, minor, axis=1)
    minor_cos = jnp.tile(minor_cos, (1, count // minor))
    minor_sin = jnp.tile(minor_sin, (1, count // minor))
    return (
        major_cos * minor_cos - major_sin * minor_sin,
        major_sin * minor_cos + major_cos * minor_sin,
    )


def shift_index(freq, count):
    signed = jnp.where(freq >= count // 2, freq - count, freq)
    return signed * (4 * RAD) // count + 2 * RAD


def split_dot(left, right):
    hi = lax.reduce_precision(left, exponent_bits=8, mantissa_bits=7)
    lo = left - hi
    return jnp.dot(hi.astype(jnp.bfloat16), right, preferred_element_type=jnp.float32) + jnp.dot(
        lo.astype(jnp.bfloat16), right, preferred_element_type=jnp.float32
    )


def on_device(frames, pixel_gain, eigen_flats, pixels):
    n_srow = lax.axis_size("srow")
    n_scol = lax.axis_size("scol")
    n_dev = n_srow * n_scol
    local_rows, local_cols, n_pix = frames.shape
    row_count = local_rows * n_srow
    col_count = local_cols * n_scol
    n_shift = 4 * RAD
    flat_index = lax.axis_index("scol") * n_srow + lax.axis_index("srow")

    readings = frames.astype(jnp.float32)
    exposure = jnp.mean(readings, axis=2, keepdims=True)
    gram = jnp.dot(eigen_flats.T, eigen_flats, precision=HIGHEST, preferred_element_type=jnp.float32)
    project = pixel_gain[:, None] * (jnp.eye(n_pix, dtype=jnp.float32) - gram)
    corrected = jnp.einsum("rcp,pq->rcq", readings, project, precision=lax.Precision.HIGH)
    flattened = (corrected / exposure).astype(jnp.bfloat16)

    gathered = lax.all_to_all(flattened, "srow", split_axis=1, concat_axis=0, tiled=True)
    cols_here = gathered.shape[1]

    k_blk = row_count // n_scol
    j_blk = col_count // n_srow
    row_ids = jnp.arange(row_count, dtype=jnp.int32)
    row_cos, row_sin = square_waves(row_count)
    forward_rows = jnp.stack([row_cos, -row_sin], axis=0).reshape(2, n_scol, k_blk, row_count)
    forward_rows = forward_rows.transpose(1, 0, 2, 3).reshape(2 * row_count, row_count)
    spec = jnp.dot(
        forward_rows.astype(jnp.bfloat16),
        gathered.reshape(row_count, cols_here * n_pix),
        preferred_element_type=jnp.float32,
    ).astype(jnp.bfloat16)
    spec = spec.reshape(n_scol, 2 * k_blk * cols_here, n_pix)

    def shift_of(freq, count):
        signed = freq - count if freq >= count // 2 else freq
        return (signed * (4 * RAD)) // count

    dx_first, dy_first = [], []
    for a in range(n_scol):
        shifts = [shift_of(k, row_count) for k in range(a * k_blk, (a + 1) * k_blk)]
        dx_first.append(min(shifts))
    n_dx = max(
        max(shift_of(k, row_count) for k in range(a * k_blk, (a + 1) * k_blk)) - dx_first[a] + 1
        for a in range(n_scol)
    )
    for b in range(n_srow):
        dy_first.append(min(shift_of(j, col_count) for j in range(b * j_blk, (b + 1) * j_blk)))
    n_dyl = max(
        max(shift_of(j, col_count) for j in range(b * j_blk, (b + 1) * j_blk)) - dy_first[b] + 1
        for b in range(n_srow)
    )
    n_dyl = -(-n_dyl // 8) * 8
    move_x = (jnp.array(dx_first, dtype=jnp.int32)[:, None] + jnp.arange(n_dx, dtype=jnp.int32)[None, :])
    move_y = (jnp.array(dy_first, dtype=jnp.int32)[:, None] + jnp.arange(n_dyl, dtype=jnp.int32)[None, :])
    move_x = move_x[:, None, None, :, None]
    move_y = move_y[None, :, :, None, None]
    det_x = (pixels % DET - DET // 2)[None, None, None, None, :]
    det_y = (pixels // DET - DET // 2)[None, None, None, None, :]
    upper = (det_x - move_x) * (det_x - move_x) + (det_y - move_y) * (det_y - move_y) <= RAD * RAD
    lower = (det_x + move_x) * (det_x + move_x) + (det_y + move_y) * (det_y + move_y) <= RAD * RAD
    weight = (upper.astype(jnp.float32) - lower.astype(jnp.float32)).astype(jnp.bfloat16)
    own_dx = (shift_index(row_ids, row_count) - 2 * RAD).reshape(n_scol, k_blk)
    own_dx = own_dx - jnp.array(dx_first, dtype=jnp.int32)[:, None]
    dx_of_n = jnp.broadcast_to(own_dx[:, None, :, None], (n_scol, 2, k_blk, cols_here))
    dx_of_n = dx_of_n.reshape(n_scol, 1, 2 * k_blk * cols_here)
    weight = weight.transpose(0, 3, 1, 2, 4).reshape(n_scol, n_dx * n_srow * n_dyl, n_pix)
    every_dx = jnp.einsum("axp,anp->axn", weight, spec, preferred_element_type=jnp.bfloat16)
    every_dx = every_dx.reshape(n_scol, n_dx, n_srow * n_dyl, 2 * k_blk * cols_here)
    dx_pick = dx_of_n[:, None, :, :] == jnp.arange(n_dx, dtype=jnp.int32)[None, :, None, None]
    summed = jnp.sum(jnp.where(dx_pick, every_dx, jnp.zeros((), jnp.bfloat16)), axis=1)
    summed = summed.reshape(n_dev, n_dyl, 2 * k_blk * cols_here).astype(jnp.bfloat16)

    summed = lax.all_to_all(summed, ("scol", "srow"), split_axis=0, concat_axis=0, tiled=True)

    a_idx = lax.axis_index("scol")
    b_idx = lax.axis_index("srow")
    col_ids = jnp.arange(col_count, dtype=jnp.int32)
    my_j = b_idx * j_blk + jnp.arange(j_blk, dtype=jnp.int32)
    src_cos, src_sin = waves(jnp.arange(n_dev, dtype=jnp.int32) * cols_here, my_j, col_count)
    by_source = jnp.dot(
        summed.reshape(n_dev, -1).T.astype(jnp.float32),
        jnp.concatenate([src_cos, src_sin], axis=1),
        precision=lax.Precision.HIGH,
        preferred_element_type=jnp.float32,
    ).reshape(n_dyl, 2, k_blk, cols_here, 2, j_blk)
    part_re = by_source[:, 0, :, :, 0] + by_source[:, 1, :, :, 1]
    part_im = by_source[:, 1, :, :, 0] - by_source[:, 0, :, :, 1]
    tw_cos, tw_sin = waves(jnp.arange(cols_here, dtype=jnp.int32), my_j, col_count)
    tw_cos = tw_cos[None, None, :, :]
    tw_sin = tw_sin[None, None, :, :]
    per_shift_re = jnp.sum(part_re * tw_cos + part_im * tw_sin, axis=2)
    per_shift_im = jnp.sum(part_im * tw_cos - part_re * tw_sin, axis=2)
    my_start = jnp.array(dy_first, dtype=jnp.int32)[b_idx]
    pick = (shift_index(my_j, col_count) - 2 * RAD - my_start)[None, :] == jnp.arange(n_dyl, dtype=jnp.int32)[:, None]
    pick = pick[:, None, :]
    psi = jnp.stack(
        [
            jnp.sum(jnp.where(pick, per_shift_re, 0.0), axis=0),
            jnp.sum(jnp.where(pick, per_shift_im, 0.0), axis=0),
        ],
        axis=1,
    )

    my_k = a_idx * k_blk + jnp.arange(k_blk, dtype=jnp.int32)
    inv_cos, inv_sin = waves(row_ids, my_k, row_count)
    inverse_rows = jnp.concatenate(
        [
            jnp.concatenate([inv_cos, -inv_sin], axis=1),
            jnp.concatenate([inv_sin, inv_cos], axis=1),
        ],
        axis=0,
    )
    inverse_rows = inverse_rows.reshape(2, n_scol, row_count // n_scol, 2 * k_blk).transpose(1, 0, 2, 3)
    inverse_rows = inverse_rows.reshape(2 * row_count, 2 * k_blk)
    psi = psi.transpose(1, 0, 2).reshape(2 * k_blk, j_blk)
    half = jnp.dot(inverse_rows, psi, precision=lax.Precision.HIGH, preferred_element_type=jnp.float32)
    half = half.reshape(n_scol, 2, row_count // n_scol, j_blk)
    half = lax.all_to_all(half.astype(jnp.bfloat16), "scol", split_axis=0, concat_axis=0, tiled=True)
    half = jnp.sum(half.astype(jnp.float32), axis=0)
    out_rows = half.shape[1]

    out_cols = col_count // n_srow
    inv_cos, inv_sin = waves(my_j, col_ids, col_count)
    inverse_cols = jnp.concatenate(
        [
            jnp.concatenate([inv_cos, inv_sin], axis=1),
            jnp.concatenate([-inv_sin, inv_cos], axis=1),
        ],
        axis=0,
    )
    half = half.transpose(1, 0, 2).reshape(out_rows, 2 * j_blk)
    image = jnp.dot(half, inverse_cols, precision=lax.Precision.HIGH, preferred_element_type=jnp.float32)
    image = image.reshape(out_rows, 2, n_srow, out_cols).transpose(2, 0, 1, 3)
    image = lax.all_to_all(image.astype(jnp.bfloat16), "srow", split_axis=0, concat_axis=0, tiled=True)
    image = jnp.sum(image.astype(jnp.float32), axis=0) * (1.0 / (row_count * col_count))
    return image


def solution(mesh):
    placed = (P("srow", "scol", None), P(), P(), P())
    return jax.shard_map(
        on_device, mesh=mesh, in_specs=placed, out_specs=P("scol", None, "srow"), check_vma=False
    )
```

```python
import math

import jax
import jax.numpy as jnp
from jax import lax
from jax.sharding import PartitionSpec as P

DET = 32
RAD = 13
HIGHEST = lax.Precision.HIGHEST


def waves(left_ids, right_ids, length):
    product = left_ids[:, None] * right_ids[None, :] % length
    phases = product.astype(jnp.float32) * (2.0 * math.pi / length)
    return (jnp.cos(phases), jnp.sin(phases))


def square_waves(count):
    minor = min(128, count)
    ids = jnp.arange(count, dtype=jnp.int32)
    major_cos, major_sin = waves(ids, jnp.arange(count // minor, dtype=jnp.int32) * minor, count)
    minor_cos, minor_sin = waves(ids, jnp.arange(minor, dtype=jnp.int32), count)
    major_cos = jnp.repeat(major_cos, minor, axis=1)
    major_sin = jnp.repeat(major_sin, minor, axis=1)
    minor_cos = jnp.tile(minor_cos, (1, count // minor))
    minor_sin = jnp.tile(minor_sin, (1, count // minor))
    return (
        major_cos * minor_cos - major_sin * minor_sin,
        major_sin * minor_cos + major_cos * minor_sin,
    )


def shift_index(freq, count):
    signed = jnp.where(freq >= count // 2, freq - count, freq)
    return signed * (4 * RAD) // count + 2 * RAD


def split_dot(left, right):
    hi = lax.reduce_precision(left, exponent_bits=8, mantissa_bits=7)
    lo = left - hi
    return jnp.dot(hi.astype(jnp.bfloat16), right, preferred_element_type=jnp.float32) + jnp.dot(
        lo.astype(jnp.bfloat16), right, preferred_element_type=jnp.float32
    )


def on_device(frames, pixel_gain, eigen_flats, pixels):
    n_srow = lax.axis_size("srow")
    n_scol = lax.axis_size("scol")
    n_dev = n_srow * n_scol
    local_rows, local_cols, n_pix = frames.shape
    row_count = local_rows * n_srow
    col_count = local_cols * n_scol
    n_shift = 4 * RAD
    flat_index = lax.axis_index("scol") * n_srow + lax.axis_index("srow")

    readings = frames.astype(jnp.float32)
    exposure = jnp.mean(readings, axis=2, keepdims=True)
    gram = jnp.dot(eigen_flats.T, eigen_flats, precision=HIGHEST, preferred_element_type=jnp.float32)
    project = pixel_gain[:, None] * (jnp.eye(n_pix, dtype=jnp.float32) - gram)
    corrected = jnp.einsum("rcp,pq->rcq", readings, project, precision=lax.Precision.HIGH)
    flattened = (corrected / exposure).astype(jnp.bfloat16)

    gathered = lax.all_to_all(flattened, "srow", split_axis=1, concat_axis=0, tiled=True)
    cols_here = gathered.shape[1]

    k_blk = row_count // n_scol
    j_blk = col_count // n_srow
    row_ids = jnp.arange(row_count, dtype=jnp.int32)
    row_cos, row_sin = square_waves(row_count)
    forward_rows = jnp.stack([row_cos, -row_sin], axis=0).reshape(2, n_scol, k_blk, row_count)
    forward_rows = forward_rows.transpose(1, 0, 2, 3).reshape(2 * row_count, row_count)
    spec = jnp.dot(
        forward_rows.astype(jnp.bfloat16),
        gathered.reshape(row_count, cols_here * n_pix),
        preferred_element_type=jnp.float32,
    ).astype(jnp.bfloat16)
    spec = spec.reshape(n_scol, 2 * k_blk * cols_here, n_pix)

    def shift_of(freq, count):
        signed = freq - count if freq >= count // 2 else freq
        return (signed * (4 * RAD)) // count

    dx_first, dy_first = [], []
    for a in range(n_scol):
        shifts = [shift_of(k, row_count) for k in range(a * k_blk, (a + 1) * k_blk)]
        dx_first.append(min(shifts))
    n_dx = max(
        max(shift_of(k, row_count) for k in range(a * k_blk, (a + 1) * k_blk)) - dx_first[a] + 1
        for a in range(n_scol)
    )
    for b in range(n_srow):
        dy_first.append(min(shift_of(j, col_count) for j in range(b * j_blk, (b + 1) * j_blk)))
    n_dyl = max(
        max(shift_of(j, col_count) for j in range(b * j_blk, (b + 1) * j_blk)) - dy_first[b] + 1
        for b in range(n_srow)
    )
    n_dyl = -(-n_dyl // 8) * 8
    move_x = (jnp.array(dx_first, dtype=jnp.int32)[:, None] + jnp.arange(n_dx, dtype=jnp.int32)[None, :])
    move_y = (jnp.array(dy_first, dtype=jnp.int32)[:, None] + jnp.arange(n_dyl, dtype=jnp.int32)[None, :])
    move_x = move_x[:, None, None, :, None]
    move_y = move_y[None, :, :, None, None]
    det_x = (pixels % DET - DET // 2)[None, None, None, None, :]
    det_y = (pixels // DET - DET // 2)[None, None, None, None, :]
    upper = (det_x - move_x) * (det_x - move_x) + (det_y - move_y) * (det_y - move_y) <= RAD * RAD
    lower = (det_x + move_x) * (det_x + move_x) + (det_y + move_y) * (det_y + move_y) <= RAD * RAD
    weight = (upper.astype(jnp.float32) - lower.astype(jnp.float32)).astype(jnp.bfloat16)
    own_dx = (shift_index(row_ids, row_count) - 2 * RAD).reshape(n_scol, k_blk)
    own_dx = own_dx - jnp.array(dx_first, dtype=jnp.int32)[:, None]
    dx_of_n = jnp.broadcast_to(own_dx[:, None, :, None], (n_scol, 2, k_blk, cols_here))
    dx_of_n = dx_of_n.reshape(n_scol, 1, 2 * k_blk * cols_here)
    weight = weight.transpose(0, 3, 1, 2, 4).reshape(n_scol, n_dx * n_srow * n_dyl, n_pix)
    every_dx = jnp.einsum("axp,anp->axn", weight, spec, preferred_element_type=jnp.bfloat16)
    every_dx = every_dx.reshape(n_scol, n_dx, n_srow * n_dyl, 2 * k_blk * cols_here)
    dx_pick = dx_of_n[:, None, :, :] == jnp.arange(n_dx, dtype=jnp.int32)[None, :, None, None]
    summed = jnp.sum(jnp.where(dx_pick, every_dx, jnp.zeros((), jnp.bfloat16)), axis=1)
    summed = summed.reshape(n_dev, n_dyl, 2 * k_blk * cols_here).astype(jnp.bfloat16)

    summed = lax.all_to_all(summed, ("scol", "srow"), split_axis=0, concat_axis=0, tiled=True)

    a_idx = lax.axis_index("scol")
    b_idx = lax.axis_index("srow")
    col_ids = jnp.arange(col_count, dtype=jnp.int32)
    my_j = b_idx * j_blk + jnp.arange(j_blk, dtype=jnp.int32)
    src_cos, src_sin = waves(jnp.arange(n_dev, dtype=jnp.int32) * cols_here, my_j, col_count)
    src_table = jnp.concatenate([src_cos, src_sin], axis=1)
    table_hi = lax.reduce_precision(src_table, exponent_bits=8, mantissa_bits=7)
    table_lo = (src_table - table_hi).astype(jnp.bfloat16)
    received = summed.reshape(n_dev, -1).T
    by_source = (
        jnp.dot(received, table_hi.astype(jnp.bfloat16), preferred_element_type=jnp.float32)
        + jnp.dot(received, table_lo, preferred_element_type=jnp.float32)
    ).reshape(n_dyl, 2, k_blk, cols_here, 2, j_blk)
    part_re = by_source[:, 0, :, :, 0] + by_source[:, 1, :, :, 1]
    part_im = by_source[:, 1, :, :, 0] - by_source[:, 0, :, :, 1]
    tw_cos, tw_sin = waves(jnp.arange(cols_here, dtype=jnp.int32), my_j, col_count)
    tw_cos = tw_cos[None, None, :, :]
    tw_sin = tw_sin[None, None, :, :]
    per_shift_re = jnp.sum(part_re * tw_cos + part_im * tw_sin, axis=2)
    per_shift_im = jnp.sum(part_im * tw_cos - part_re * tw_sin, axis=2)
    my_start = jnp.array(dy_first, dtype=jnp.int32)[b_idx]
    pick = (shift_index(my_j, col_count) - 2 * RAD - my_start)[None, :] == jnp.arange(n_dyl, dtype=jnp.int32)[:, None]
    pick = pick[:, None, :]
    psi = jnp.stack(
        [
            jnp.sum(jnp.where(pick, per_shift_re, 0.0), axis=0),
            jnp.sum(jnp.where(pick, per_shift_im, 0.0), axis=0),
        ],
        axis=1,
    )

    my_k = a_idx * k_blk + jnp.arange(k_blk, dtype=jnp.int32)
    inv_cos, inv_sin = waves(row_ids, my_k, row_count)
    inverse_rows = jnp.concatenate(
        [
            jnp.concatenate([inv_cos, -inv_sin], axis=1),
            jnp.concatenate([inv_sin, inv_cos], axis=1),
        ],
        axis=0,
    )
    psi = psi.transpose(1, 0, 2).reshape(2 * k_blk, j_blk)
    half = jnp.dot(inverse_rows, psi, precision=lax.Precision.HIGH, preferred_element_type=jnp.float32)
    half = half.reshape(2, n_scol, row_count // n_scol, j_blk).transpose(1, 0, 2, 3)
    half = lax.all_to_all(half.astype(jnp.bfloat16), "scol", split_axis=0, concat_axis=0, tiled=True)
    half = jnp.sum(half.astype(jnp.float32), axis=0)
    out_rows = half.shape[1]

    out_cols = col_count // n_srow
    inv_cos, inv_sin = waves(my_j, col_ids, col_count)
    inverse_cols = jnp.concatenate(
        [
            jnp.concatenate([inv_cos, inv_sin], axis=1),
            jnp.concatenate([-inv_sin, inv_cos], axis=1),
        ],
        axis=0,
    )
    half = half.transpose(1, 0, 2).reshape(out_rows, 2 * j_blk)
    image = jnp.dot(half, inverse_cols, precision=lax.Precision.HIGH, preferred_element_type=jnp.float32)
    image = image.reshape(out_rows, 2, n_srow, out_cols).transpose(2, 0, 1, 3)
    image = lax.all_to_all(image.astype(jnp.bfloat16), "srow", split_axis=0, concat_axis=0, tiled=True)
    image = jnp.sum(image.astype(jnp.float32), axis=0) * (1.0 / (row_count * col_count))
    return image


def solution(mesh):
    placed = (P("srow", "scol", None), P(), P(), P())
    return jax.shard_map(
        on_device, mesh=mesh, in_specs=placed, out_specs=P("scol", None, "srow"), check_vma=False
    )
```
